512 devices in a mesh: panel: 16 (over y_hi, x), tile: 32 (over z, y_lo, core).
Axes of the slice: x: 4, y: 8 (y_hi: 4, y_lo: 2; y = y_hi * 2 + y_lo), z: 8, core: 2. Of those that a mesh axis runs over, the one named last changes fastest.
Arguments:
- tracer: bfloat16 [144, 768, 1152], P('panel', 'tile'), may hold values from 0.099609375 to 2
- moments: float32 [2, 144, 768, 4, 6], P(None, 'panel', 'tile'), may hold values from -0.9 to 0.9
- pieces: int32 [2, 144, 768, 4], P(None, 'panel', 'tile'), may hold values from 0 to 11
- cell_area: float32 [144, 768], P('panel', 'tile'), may hold values from 0.5 to 2
Outputs:
- updated: bfloat16 [144, 768, 1152], P('panel', 'tile')
The draws below stay inside these ranges and needn't reach their ends.
Inputs may be any that keep to these rules, and one draw needn't show every extreme that they name: Codes of the cells that a face's swept pieces intersect.
All inputs are finite; a program needn't handle non-finite values.
Results may differ from the reference program's by a relative error of at most 0.0018.
Values may be sent and summed in bfloat16 or wider, within the bound.
No kernel may reach another device: no remote copies, remote signals or barrier semaphores. Data moves between devices by JAX's collectives and lax.ppermute only.
A program may use at most 64 MiB of HBM per device.

```python
import math
import jax
import jax.numpy as jnp
import numpy as np
from jax import lax

CELL_ROWS = 9
PIECES = 4
COLUMNS = 1152
NROWS = 144
NCOLS = 768
N_PANEL = 16


def plant(result, own_key, smallest, high):
    longest = result.shape.index(max(result.shape))
    spots = []
    for shift in (0, 1):
        where = [jax.random.randint(jax.random.fold_in(own_key, axis), (), 0, length) for axis, length in enumerate(result.shape)]
        where[longest] = (where[longest] + shift) % result.shape[longest]
        spots.append(tuple(where))
    return result.at[spots[0]].set(smallest).at[spots[1]].set(high)


def steps_of(stream_key, shape, cuts, least, high):
    loudness = 1.0
    for dim, parts in cuts:
        steps = jax.random.uniform(jax.random.fold_in(jax.random.fold_in(stream_key, 6), dim), (parts,), jnp.float32, least / len(cuts), high / len(cuts))
        loudness = loudness * jnp.repeat(jnp.exp(steps), shape[dim] // parts).reshape((-1,) + (1,) * (len(shape) - 1 - dim))
    return loudness


def gaussian(key, dims, deviation, bound, split=(), kind=jnp.bfloat16):
    factor_of = steps_of(key, dims, split, -0.22, 0.18) if split else 1.0
    result = jax.random.normal(key, dims, jnp.float32) * deviation * factor_of
    return jnp.minimum(jnp.maximum(result, -bound), bound).astype(kind)


def setup_inputs(seed: int = 0) -> dict:
    streams_of = jax.random.split(jax.random.key(seed), 5)
    return {
        "tracer": jnp.clip(0.099609375 + 1.9003906 * jax.random.uniform(streams_of[0], (NROWS, NCOLS, COLUMNS), jnp.float32) ** steps_of(streams_of[0], (NROWS, NCOLS, COLUMNS), ((0, 16), (1, 32)), -0.2, 0.2), 0.099609375, 2.0).astype(jnp.bfloat16),
        "moments": gaussian(streams_of[1], (2, NROWS, NCOLS, PIECES, 6), 0.15, 0.9, ((1, 16), (2, 32)), jnp.float32),
        "pieces": plant(jax.random.randint(streams_of[2], (2, NROWS, NCOLS, PIECES), 0, 12), jax.random.fold_in(streams_of[2], 1), 0, 11).astype(jnp.int32),
        "cell_area": jnp.clip(jnp.exp(math.log(2.0) - 1.3862944 * jax.random.uniform(streams_of[3], (NROWS, NCOLS), jnp.float32) ** steps_of(streams_of[3], (NROWS, NCOLS), ((0, 16), (1, 32)), -0.2, 0.2)), 0.5, 2.0),
    }


def stencil_table():
    stencil = np.zeros((6, 3, 3))
    stencil[0, 1, 1] = 7.0 / 6.0
    stencil[0, 1, 0] = -1.0 / 24.0
    stencil[0, 1, 2] = -1.0 / 24.0
    stencil[0, 0, 1] = -1.0 / 24.0
    stencil[0, 2, 1] = -1.0 / 24.0
    stencil[1, 1, 2] = 0.5
    stencil[1, 1, 0] = -0.5
    stencil[2, 2, 1] = 0.5
    stencil[2, 0, 1] = -0.5
    stencil[3, 1, 2] = 0.5
    stencil[3, 1, 0] = 0.5
    stencil[3, 1, 1] = -1.0
    stencil[4, 2, 2] = 0.25
    stencil[4, 2, 0] = -0.25
    stencil[4, 0, 2] = -0.25
    stencil[4, 0, 0] = 0.25
    stencil[5, 2, 1] = 0.5
    stencil[5, 0, 1] = 0.5
    stencil[5, 1, 1] = -1.0
    return stencil


def tap_tables():
    stencil = stencil_table()
    tables = np.zeros((2, 12, 6, 36))
    for direction in range(2):
        for code in range(12):
            if direction == 0:
                row_off = code // 4 - 1
                col_off = code % 4 - 1
            else:
                row_off = code % 4 - 1
                col_off = code // 4 - 1
            for tap_index in range(36):
                inner_row = tap_index // 6 - 2 - row_off
                inner_col = tap_index % 6 - 2 - col_off
                if abs(inner_row) <= 1 and abs(inner_col) <= 1:
                    tables[direction, code, :, tap_index] = stencil[:, inner_row + 1, inner_col + 1]
    return tables


def compose_taps(pieces, moments):
    codes = jnp.arange(12, dtype=jnp.int32)
    onehot = (pieces[..., None] == codes).astype(jnp.float32)
    summed = jnp.einsum("dijko,dijkm->dijom", onehot, moments, precision=lax.Precision.HIGHEST)
    tables = jnp.asarray(tap_tables(), dtype=jnp.float32)
    return jnp.einsum("dijom,domt->dijt", summed, tables, precision=lax.Precision.HIGHEST)


def apply_taps(weights, padded, row_start, col_start, nrow, ncol):
    width = padded.shape[2]
    total = jnp.zeros((nrow, ncol, width), jnp.float32)
    for tap_index in range(36):
        tap_row = row_start + tap_index // 6 - 2
        tap_col = col_start + tap_index % 6 - 2
        piece = lax.slice(padded, (tap_row, tap_col, 0), (tap_row + nrow, tap_col + ncol, width))
        total = total + weights[:, :, tap_index][:, :, None] * piece.astype(jnp.float32)
    return total


def reference(tracer, moments, pieces, cell_area):
    weights = compose_taps(pieces, moments)
    row_mask = jnp.where(jnp.arange(NROWS) == NROWS - 1, 0.0, 1.0).astype(jnp.float32)
    east_weights = weights[0]
    north_weights = weights[1] * row_mask[:, None, None]
    north_weights = jnp.pad(north_weights, ((1, 0), (0, 0), (0, 0)))
    padded = jnp.pad(tracer, ((3, 3), (0, 0), (0, 0)))
    padded = jnp.concatenate([padded[:, NCOLS - 3:], padded, padded[:, :3]], axis=1)

    def one_band(band):
        start = band * CELL_ROWS
        block = lax.dynamic_slice_in_dim(padded, start, CELL_ROWS + 6, 0)
        east_part = lax.dynamic_slice_in_dim(east_weights, start, CELL_ROWS, 0)
        north_part = lax.dynamic_slice_in_dim(north_weights, start, CELL_ROWS + 1, 0)
        east = apply_taps(east_part, block, 3, 3, CELL_ROWS, NCOLS)
        north_all = apply_taps(north_part, block, 2, 3, CELL_ROWS + 1, NCOLS)
        west = jnp.roll(east, 1, axis=1)
        south = north_all[:-1]
        north = north_all[1:]
        tracer_part = lax.dynamic_slice_in_dim(tracer, start, CELL_ROWS, 0)
        area_part = lax.dynamic_slice_in_dim(cell_area, start, CELL_ROWS, 0)
        change = ((west - east) + (south - north)) / area_part[:, :, None]
        return (tracer_part.astype(jnp.float32) + change).astype(jnp.bfloat16)

    bands = lax.map(one_band, jnp.arange(N_PANEL, dtype=jnp.int32))
    return bands.reshape(NROWS, NCOLS, COLUMNS)
```

```python
import jax
import jax.numpy as jnp
import numpy as np
from jax import lax
from jax.sharding import PartitionSpec as P


def from_prev(value, axis, wrap):
    size = lax.axis_size(axis)
    pairs = [(i, (i + 1) % size) for i in range(size if wrap else size - 1)]
    return lax.ppermute(value, axis, pairs)


def from_next(value, axis, wrap):
    size = lax.axis_size(axis)
    pairs = [((i + 1) % size, i) for i in range(size if wrap else size - 1)]
    return lax.ppermute(value, axis, pairs)


def stencil_table():
    stencil = np.zeros((6, 3, 3))
    stencil[0, 1, 1] = 7.0 / 6.0
    stencil[0, 1, 0] = -1.0 / 24.0
    stencil[0, 1, 2] = -1.0 / 24.0
    stencil[0, 0, 1] = -1.0 / 24.0
    stencil[0, 2, 1] = -1.0 / 24.0
    stencil[1, 1, 2] = 0.5
    stencil[1, 1, 0] = -0.5
    stencil[2, 2, 1] = 0.5
    stencil[2, 0, 1] = -0.5
    stencil[3, 1, 2] = 0.5
    stencil[3, 1, 0] = 0.5
    stencil[3, 1, 1] = -1.0
    stencil[4, 2, 2] = 0.25
    stencil[4, 2, 0] = -0.25
    stencil[4, 0, 2] = -0.25
    stencil[4, 0, 0] = 0.25
    stencil[5, 2, 1] = 0.5
    stencil[5, 0, 1] = 0.5
    stencil[5, 1, 1] = -1.0
    return stencil


def face_tables():
    stencil = stencil_table()
    tables = np.zeros((4, 12, 6, 7, 7))
    for face, (direction, shift_row, shift_col, sign) in enumerate(
        ((0, 0, -1, 1.0), (0, 0, 0, -1.0), (1, -1, 0, 1.0), (1, 0, 0, -1.0))
    ):
        for code in range(12):
            if direction == 0:
                row_off, col_off = code // 4 - 1, code % 4 - 1
            else:
                row_off, col_off = code % 4 - 1, code // 4 - 1
            for inner_row in range(-1, 2):
                for inner_col in range(-1, 2):
                    r = row_off + inner_row + shift_row + 3
                    c = col_off + inner_col + shift_col + 3
                    tables[face, code, :, r, c] += sign * stencil[:, inner_row + 1, inner_col + 1]
    tables = tables.reshape(4, 12, 6, 49)
    used = np.nonzero(np.abs(tables).sum(axis=(0, 1, 2)) > 0)[0]
    return tables[..., used], [(int(t) // 7 - 3, int(t) % 7 - 3) for t in used]


def summed_moments(pieces, moments):
    codes = jnp.arange(12, dtype=jnp.int32)
    onehot = (pieces[..., None] == codes).astype(jnp.float32)
    return jnp.einsum("ijko,ijkm->ijom", onehot, moments, precision=lax.Precision.HIGHEST)


def local(tracer, moments, pieces, cell_area):
    rows = tracer.shape[0]
    cols = tracer.shape[1]
    tables, offsets = face_tables()

    packed = jnp.concatenate([moments, pieces.astype(jnp.float32)[..., None]], axis=-1)
    west_col = from_prev(packed[0][:, cols - 1 :], "tile", True)
    south_row = from_prev(packed[1][rows - 1 :], "panel", False)

    wide = jnp.concatenate(
        [from_prev(tracer[:, cols - 3 :], "tile", True), tracer, from_next(tracer[:, :3], "tile", True)], axis=1
    )
    padded = jnp.concatenate(
        [from_prev(wide[rows - 3 :], "panel", False), wide, from_next(wide[:3], "panel", False)], axis=0
    )

    east_in = jnp.concatenate([west_col, packed[0]], axis=1)
    north_in = jnp.concatenate([south_row, packed[1]], axis=0)
    east_sum = summed_moments(east_in[..., 6].astype(jnp.int32), east_in[..., :6])
    north_sum = summed_moments(north_in[..., 6].astype(jnp.int32), north_in[..., :6])
    is_top = lax.axis_index("panel") == lax.axis_size("panel") - 1
    last_row = jnp.arange(rows + 1) == rows
    row_mask = jnp.where(jnp.logical_and(last_row, is_top), 0.0, 1.0).astype(jnp.float32)
    north_sum = north_sum * row_mask[:, None, None, None]

    faces = jnp.stack(
        [east_sum[:, :cols], east_sum[:, 1:], north_sum[:rows], north_sum[1:]], axis=2
    )
    weights = jnp.einsum(
        "ijfcm,fcmt->ijt", faces, jnp.asarray(tables, jnp.float32), precision=lax.Precision.HIGHEST
    )
    weights = weights / cell_area[:, :, None]

    total = tracer.astype(jnp.float32)
    for tap, (dr, dc) in enumerate(offsets):
        piece = lax.slice(padded, (3 + dr, 3 + dc, 0), (3 + dr + rows, 3 + dc + cols, padded.shape[2]))
        total = total + weights[:, :, tap][:, :, None] * piece.astype(jnp.float32)
    return total.astype(jnp.bfloat16)


def solution(mesh):
    in_specs = (
        P("panel", "tile", None),
        P(None, "panel", "tile", None, None),
        P(None, "panel", "tile", None),
        P("panel", "tile"),
    )
    out_specs = P("panel", "tile", None)
    return jax.shard_map(local, mesh=mesh, in_specs=in_specs, out_specs=out_specs, check_vma=False)
```

```python
import jax
import jax.numpy as jnp
import numpy as np
from jax import lax
from jax.sharding import PartitionSpec as P


def from_prev(value, axis, wrap):
    size = lax.axis_size(axis)
    pairs = [(i, (i + 1) % size) for i in range(size if wrap else size - 1)]
    return lax.ppermute(value, axis, pairs)


def from_next(value, axis, wrap):
    size = lax.axis_size(axis)
    pairs = [((i + 1) % size, i) for i in range(size if wrap else size - 1)]
    return lax.ppermute(value, axis, pairs)


def stencil_table():
    stencil = np.zeros((6, 3, 3))
    stencil[0, 1, 1] = 7.0 / 6.0
    stencil[0, 1, 0] = -1.0 / 24.0
    stencil[0, 1, 2] = -1.0 / 24.0
    stencil[0, 0, 1] = -1.0 / 24.0
    stencil[0, 2, 1] = -1.0 / 24.0
    stencil[1, 1, 2] = 0.5
    stencil[1, 1, 0] = -0.5
    stencil[2, 2, 1] = 0.5
    stencil[2, 0, 1] = -0.5
    stencil[3, 1, 2] = 0.5
    stencil[3, 1, 0] = 0.5
    stencil[3, 1, 1] = -1.0
    stencil[4, 2, 2] = 0.25
    stencil[4, 2, 0] = -0.25
    stencil[4, 0, 2] = -0.25
    stencil[4, 0, 0] = 0.25
    stencil[5, 2, 1] = 0.5
    stencil[5, 0, 1] = 0.5
    stencil[5, 1, 1] = -1.0
    return stencil


def face_tables():
    stencil = stencil_table()
    tables = np.zeros((4, 12, 6, 7, 7))
    for face, (direction, shift_row, shift_col, sign) in enumerate(
        ((0, 0, -1, 1.0), (0, 0, 0, -1.0), (1, -1, 0, 1.0), (1, 0, 0, -1.0))
    ):
        for code in range(12):
            if direction == 0:
                row_off, col_off = code // 4 - 1, code % 4 - 1
            else:
                row_off, col_off = code % 4 - 1, code // 4 - 1
            for inner_row in range(-1, 2):
                for inner_col in range(-1, 2):
                    r = row_off + inner_row + shift_row + 3
                    c = col_off + inner_col + shift_col + 3
                    tables[face, code, :, r, c] += sign * stencil[:, inner_row + 1, inner_col + 1]
    tables = tables.reshape(4, 12, 6, 49)
    used = np.nonzero(np.abs(tables).sum(axis=(0, 1, 2)) > 0)[0]
    return tables[..., used], [(int(t) // 7 - 3, int(t) % 7 - 3) for t in used]


def summed_moments(pieces, moments):
    codes = jnp.arange(12, dtype=jnp.int32)
    onehot = (pieces[..., None] == codes).astype(jnp.float32)
    return jnp.einsum("ijko,ijkm->ijom", onehot, moments, precision=lax.Precision.HIGHEST)


def split3(value):
    hi = value.astype(jnp.bfloat16)
    rest = value - hi.astype(jnp.float32)
    mid = rest.astype(jnp.bfloat16)
    lo = (rest - mid.astype(jnp.float32)).astype(jnp.bfloat16)
    return jnp.concatenate([hi, mid, lo], axis=-1)


def join3(value, count):
    parts = [value[..., k * count : (k + 1) * count].astype(jnp.float32) for k in range(3)]
    return (parts[0] + parts[1]) + parts[2]


def pack_weights(moments, pieces, width):
    lead = moments.shape[:-2]
    flat = moments.reshape(lead + (moments.shape[-2] * moments.shape[-1],))
    packed = jnp.concatenate([split3(flat), pieces.astype(jnp.bfloat16)], axis=-1)
    return jnp.pad(packed, [(0, 0)] * len(lead) + [(0, width - packed.shape[-1])])


def unpack_weights(packed, n_piece, n_moment):
    count = n_piece * n_moment
    lead = packed.shape[:-1]
    moments = join3(packed[..., : 3 * count], count).reshape(lead + (n_piece, n_moment))
    pieces = packed[..., 3 * count : 3 * count + n_piece].astype(jnp.int32)
    return moments, pieces


def local(tracer, moments, pieces, cell_area):
    rows = tracer.shape[0]
    cols = tracer.shape[1]
    width = tracer.shape[2]
    n_piece = moments.shape[3]
    n_moment = moments.shape[4]
    tables, offsets = face_tables()

    west_pack = pack_weights(moments[0][:, cols - 1], pieces[0][:, cols - 1], width)[:, None]
    south_pack = pack_weights(moments[1][rows - 1], pieces[1][rows - 1], width)[None]
    from_west = from_prev(jnp.concatenate([tracer[:, cols - 3 :], west_pack], axis=1), "tile", True)
    from_east = from_next(tracer[:, :3], "tile", True)
    from_south = from_prev(jnp.concatenate([tracer[rows - 3 :], south_pack], axis=0), "panel", False)
    from_north = from_next(tracer[:3], "panel", False)

    west_halo = from_west[:, :3]
    corners_up = jnp.concatenate([west_halo[rows - 3 :], from_east[rows - 3 :]], axis=1)
    corners_down = jnp.concatenate([west_halo[:3], from_east[:3]], axis=1)
    south_corners = from_prev(corners_up, "panel", False)
    north_corners = from_next(corners_down, "panel", False)

    wide = jnp.concatenate([west_halo, tracer, from_east], axis=1)
    south_rows = jnp.concatenate([south_corners[:, :3], from_south[:3], south_corners[:, 3:]], axis=1)
    north_rows = jnp.concatenate([north_corners[:, :3], from_north, north_corners[:, 3:]], axis=1)
    padded = jnp.concatenate([south_rows, wide, north_rows], axis=0)

    west_m, west_p = unpack_weights(from_west[:, 3], n_piece, n_moment)
    south_m, south_p = unpack_weights(from_south[3], n_piece, n_moment)
    east_sum = summed_moments(
        jnp.concatenate([west_p[:, None], pieces[0]], axis=1),
        jnp.concatenate([west_m[:, None], moments[0]], axis=1),
    )
    north_sum = summed_moments(
        jnp.concatenate([south_p[None], pieces[1]], axis=0),
        jnp.concatenate([south_m[None], moments[1]], axis=0),
    )
    is_top = lax.axis_index("panel") == lax.axis_size("panel") - 1
    last_row = jnp.arange(rows + 1) == rows
    row_mask = jnp.where(jnp.logical_and(last_row, is_top), 0.0, 1.0).astype(jnp.float32)
    north_sum = north_sum * row_mask[:, None, None, None]

    faces = jnp.stack(
        [east_sum[:, :cols], east_sum[:, 1:], north_sum[:rows], north_sum[1:]], axis=2
    )
    weights = jnp.einsum(
        "ijfcm,fcmt->ijt", faces, jnp.asarray(tables, jnp.float32), precision=lax.Precision.HIGHEST
    )
    weights = weights / cell_area[:, :, None]

    total = tracer.astype(jnp.float32)
    for tap, (dr, dc) in enumerate(offsets):
        piece = lax.slice(padded, (3 + dr, 3 + dc, 0), (3 + dr + rows, 3 + dc + cols, width))
        total = total + weights[:, :, tap][:, :, None] * piece.astype(jnp.float32)
    return total.astype(jnp.bfloat16)


def solution(mesh):
    in_specs = (
        P("panel", "tile", None),
        P(None, "panel", "tile", None, None),
        P(None, "panel", "tile", None),
        P("panel", "tile"),
    )
    out_specs = P("panel", "tile", None)
    return jax.shard_map(local, mesh=mesh, in_specs=in_specs, out_specs=out_specs, check_vma=False)
```

```python
import jax
import jax.numpy as jnp
import numpy as np
from jax import lax
from jax.sharding import PartitionSpec as P


def from_prev(value, axis, wrap):
    size = lax.axis_size(axis)
    pairs = [(i, (i + 1) % size) for i in range(size if wrap else size - 1)]
    return lax.ppermute(value, axis, pairs)


def from_next(value, axis, wrap):
    size = lax.axis_size(axis)
    pairs = [((i + 1) % size, i) for i in range(size if wrap else size - 1)]
    return lax.ppermute(value, axis, pairs)


def stencil_table():
    stencil = np.zeros((6, 3, 3))
    stencil[0, 1, 1] = 7.0 / 6.0
    stencil[0, 1, 0] = -1.0 / 24.0
    stencil[0, 1, 2] = -1.0 / 24.0
    stencil[0, 0, 1] = -1.0 / 24.0
    stencil[0, 2, 1] = -1.0 / 24.0
    stencil[1, 1, 2] = 0.5
    stencil[1, 1, 0] = -0.5
    stencil[2, 2, 1] = 0.5
    stencil[2, 0, 1] = -0.5
    stencil[3, 1, 2] = 0.5
    stencil[3, 1, 0] = 0.5
    stencil[3, 1, 1] = -1.0
    stencil[4, 2, 2] = 0.25
    stencil[4, 2, 0] = -0.25
    stencil[4, 0, 2] = -0.25
    stencil[4, 0, 0] = 0.25
    stencil[5, 2, 1] = 0.5
    stencil[5, 0, 1] = 0.5
    stencil[5, 1, 1] = -1.0
    return stencil


def face_tables():
    stencil = stencil_table()
    tables = np.zeros((4, 12, 6, 7, 7))
    for face, (direction, shift_row, shift_col, sign) in enumerate(
        ((0, 0, -1, 1.0), (0, 0, 0, -1.0), (1, -1, 0, 1.0), (1, 0, 0, -1.0))
    ):
        for code in range(12):
            if direction == 0:
                row_off, col_off = code // 4 - 1, code % 4 - 1
            else:
                row_off, col_off = code % 4 - 1, code // 4 - 1
            for inner_row in range(-1, 2):
                for inner_col in range(-1, 2):
                    r = row_off + inner_row + shift_row + 3
                    c = col_off + inner_col + shift_col + 3
                    tables[face, code, :, r, c] += sign * stencil[:, inner_row + 1, inner_col + 1]
    tables = tables.reshape(4, 12, 6, 49)
    used = np.nonzero(np.abs(tables).sum(axis=(0, 1, 2)) > 0)[0]
    return tables[..., used], [(int(t) // 7 - 3, int(t) % 7 - 3) for t in used]


def summed_moments(pieces, moments):
    codes = jnp.arange(12, dtype=jnp.int32)
    onehot = (pieces[..., None] == codes).astype(jnp.float32)
    return jnp.einsum("...ko,...km->...om", onehot, moments, precision=lax.Precision.HIGHEST)


def split3(value):
    hi = value.astype(jnp.bfloat16)
    rest = value - hi.astype(jnp.float32)
    mid = rest.astype(jnp.bfloat16)
    lo = (rest - mid.astype(jnp.float32)).astype(jnp.bfloat16)
    return jnp.concatenate([hi, mid, lo], axis=-1)


def join3(value, count):
    parts = [value[..., k * count : (k + 1) * count].astype(jnp.float32) for k in range(3)]
    return (parts[0] + parts[1]) + parts[2]


def pack_weights(moments, pieces, width):
    lead = moments.shape[:-2]
    flat = moments.reshape(lead + (moments.shape[-2] * moments.shape[-1],))
    packed = jnp.concatenate([split3(flat), pieces.astype(jnp.bfloat16)], axis=-1)
    return jnp.pad(packed, [(0, 0)] * len(lead) + [(0, width - packed.shape[-1])])


def unpack_weights(packed, n_piece, n_moment):
    count = n_piece * n_moment
    lead = packed.shape[:-1]
    moments = join3(packed[..., : 3 * count], count).reshape(lead + (n_piece, n_moment))
    pieces = packed[..., 3 * count : 3 * count + n_piece].astype(jnp.int32)
    return moments, pieces


def from_corner(value, step_panel, step_tile):
    n_panel = lax.axis_size("panel")
    n_tile = lax.axis_size("tile")
    pairs = []
    for p in range(n_panel):
        q = p + step_panel
        if 0 <= q < n_panel:
            for t in range(n_tile):
                pairs.append((p * n_tile + t, q * n_tile + (t + step_tile) % n_tile))
    return lax.ppermute(value, ("panel", "tile"), pairs)


def local(tracer, moments, pieces, cell_area):
    rows = tracer.shape[0]
    cols = tracer.shape[1]
    width = tracer.shape[2]
    n_piece = moments.shape[3]
    n_moment = moments.shape[4]
    tables, offsets = face_tables()
    tables = jnp.asarray(tables, jnp.float32)

    west_pack = pack_weights(moments[0][:, cols - 1], pieces[0][:, cols - 1], width)[:, None]
    south_pack = pack_weights(moments[1][rows - 1], pieces[1][rows - 1], width)[None]
    from_west = from_prev(jnp.concatenate([tracer[:, cols - 3 :], west_pack], axis=1), "tile", True)
    from_east = from_next(tracer[:, :3], "tile", True)
    from_south = from_prev(jnp.concatenate([tracer[rows - 3 :], south_pack], axis=0), "panel", False)
    from_north = from_next(tracer[:3], "panel", False)
    from_sw = from_corner(tracer[rows - 3 :, cols - 3 :], 1, 1)
    from_se = from_corner(tracer[rows - 3 :, :3], 1, -1)
    from_nw = from_corner(tracer[:3, cols - 3 :], -1, 1)
    from_ne = from_corner(tracer[:3, :3], -1, -1)

    south_rows = jnp.concatenate([from_sw, from_south[:3], from_se], axis=1)
    wide = jnp.concatenate([from_west[:, :3], tracer, from_east], axis=1)
    north_rows = jnp.concatenate([from_nw, from_north, from_ne], axis=1)
    padded = jnp.concatenate([south_rows, wide, north_rows], axis=0)

    is_top = lax.axis_index("panel") == lax.axis_size("panel") - 1
    last_row = jnp.arange(rows) == rows - 1
    row_mask = jnp.where(jnp.logical_and(last_row, is_top), 0.0, 1.0).astype(jnp.float32)
    east_sum = summed_moments(pieces[0], moments[0])
    north_sum = summed_moments(pieces[1], moments[1]) * row_mask[:, None, None, None]
    faces = jnp.stack(
        [
            jnp.pad(east_sum[:, : cols - 1], ((0, 0), (1, 0), (0, 0), (0, 0))),
            east_sum,
            jnp.pad(north_sum[: rows - 1], ((1, 0), (0, 0), (0, 0), (0, 0))),
            north_sum,
        ],
        axis=2,
    )
    weights = jnp.einsum("ijfcm,fcmt->ijt", faces, tables, precision=lax.Precision.HIGHEST)

    west_m, west_p = unpack_weights(from_west[:, 3], n_piece, n_moment)
    south_m, south_p = unpack_weights(from_south[3], n_piece, n_moment)
    west_fix = jnp.einsum(
        "icm,cmt->it", summed_moments(west_p, west_m), tables[0], precision=lax.Precision.HIGHEST
    )
    south_fix = jnp.einsum(
        "jcm,cmt->jt", summed_moments(south_p, south_m), tables[2], precision=lax.Precision.HIGHEST
    )
    weights = weights + jnp.pad(west_fix[:, None], ((0, 0), (0, cols - 1), (0, 0)))
    weights = weights + jnp.pad(south_fix[None], ((0, rows - 1), (0, 0), (0, 0)))
    weights = weights / cell_area[:, :, None]

    total = tracer.astype(jnp.float32)
    for tap, (dr, dc) in enumerate(offsets):
        piece = lax.slice(padded, (3 + dr, 3 + dc, 0), (3 + dr + rows, 3 + dc + cols, width))
        total = total + weights[:, :, tap][:, :, None] * piece.astype(jnp.float32)
    return total.astype(jnp.bfloat16)


def solution(mesh):
    in_specs = (
        P("panel", "tile", None),
        P(None, "panel", "tile", None, None),
        P(None, "panel", "tile", None),
        P("panel", "tile"),
    )
    out_specs = P("panel", "tile", None)
    return jax.shard_map(local, mesh=mesh, in_specs=in_specs, out_specs=out_specs, check_vma=False)
```

```python
import jax
import jax.numpy as jnp
import numpy as np
from jax import lax
from jax.sharding import PartitionSpec as P


def from_prev(value, axis, wrap):
    size = lax.axis_size(axis)
    pairs = [(i, (i + 1) % size) for i in range(size if wrap else size - 1)]
    return lax.ppermute(value, axis, pairs)


def from_next(value, axis, wrap):
    size = lax.axis_size(axis)
    pairs = [((i + 1) % size, i) for i in range(size if wrap else size - 1)]
    return lax.ppermute(value, axis, pairs)


def stencil_table():
    stencil = np.zeros((6, 3, 3))
    stencil[0, 1, 1] = 7.0 / 6.0
    stencil[0, 1, 0] = -1.0 / 24.0
    stencil[0, 1, 2] = -1.0 / 24.0
    stencil[0, 0, 1] = -1.0 / 24.0
    stencil[0, 2, 1] = -1.0 / 24.0
    stencil[1, 1, 2] = 0.5
    stencil[1, 1, 0] = -0.5
    stencil[2, 2, 1] = 0.5
    stencil[2, 0, 1] = -0.5
    stencil[3, 1, 2] = 0.5
    stencil[3, 1, 0] = 0.5
    stencil[3, 1, 1] = -1.0
    stencil[4, 2, 2] = 0.25
    stencil[4, 2, 0] = -0.25
    stencil[4, 0, 2] = -0.25
    stencil[4, 0, 0] = 0.25
    stencil[5, 2, 1] = 0.5
    stencil[5, 0, 1] = 0.5
    stencil[5, 1, 1] = -1.0
    return stencil


def face_tables():
    stencil = stencil_table()
    tables = np.zeros((4, 12, 6, 7, 7))
    for face, (direction, shift_row, shift_col, sign) in enumerate(
        ((0, 0, -1, 1.0), (0, 0, 0, -1.0), (1, -1, 0, 1.0), (1, 0, 0, -1.0))
    ):
        for code in range(12):
            if direction == 0:
                row_off, col_off = code // 4 - 1, code % 4 - 1
            else:
                row_off, col_off = code % 4 - 1, code // 4 - 1
            for inner_row in range(-1, 2):
                for inner_col in range(-1, 2):
                    r = row_off + inner_row + shift_row + 3
                    c = col_off + inner_col + shift_col + 3
                    tables[face, code, :, r, c] += sign * stencil[:, inner_row + 1, inner_col + 1]
    tables = tables.reshape(4, 12, 6, 49)
    used = np.nonzero(np.abs(tables).sum(axis=(0, 1, 2)) > 0)[0]
    return tables[..., used], [(int(t) // 7 - 3, int(t) % 7 - 3) for t in used]


def summed_moments(pieces, moments):
    codes = jnp.arange(12, dtype=jnp.int32)
    onehot = (pieces[..., None] == codes).astype(jnp.float32)
    return jnp.einsum("...ko,...km->...om", onehot, moments, precision=lax.Precision.HIGHEST)


def split3(value):
    hi = lax.reduce_precision(value, exponent_bits=8, mantissa_bits=7)
    rest = value - hi
    mid = lax.reduce_precision(rest, exponent_bits=8, mantissa_bits=7)
    lo = rest - mid
    return jnp.concatenate([hi, mid, lo], axis=-1).astype(jnp.bfloat16)


def join3(value, count):
    parts = [value[..., k * count : (k + 1) * count].astype(jnp.float32) for k in range(3)]
    return (parts[0] + parts[1]) + parts[2]


def pack_weights(moments, pieces, width):
    lead = moments.shape[:-2]
    flat = moments.reshape(lead + (moments.shape[-2] * moments.shape[-1],))
    packed = jnp.concatenate([split3(flat), pieces.astype(jnp.bfloat16)], axis=-1)
    return jnp.pad(packed, [(0, 0)] * len(lead) + [(0, width - packed.shape[-1])])


def unpack_weights(packed, n_piece, n_moment):
    count = n_piece * n_moment
    lead = packed.shape[:-1]
    moments = join3(packed[..., : 3 * count], count).reshape(lead + (n_piece, n_moment))
    pieces = packed[..., 3 * count : 3 * count + n_piece].astype(jnp.int32)
    return moments, pieces


def face_weights(moments, pieces, tables):
    n_code = tables.shape[1]
    onehot = (pieces[..., None] == jnp.arange(n_code, dtype=jnp.int32)).astype(jnp.float32)
    spread = jnp.sum(onehot[..., :, None] * moments[..., None, :], axis=-3)
    lead = spread.shape[:-3]
    flat = spread.reshape(lead + (-1,))
    return jnp.dot(flat, tables.reshape(-1, tables.shape[-1]), precision=lax.Precision.HIGHEST)


def local(tracer, moments, pieces, cell_area):
    rows = tracer.shape[0]
    cols = tracer.shape[1]
    width = tracer.shape[2]
    n_piece = moments.shape[3]
    n_moment = moments.shape[4]
    tables, offsets = face_tables()
    tables = jnp.asarray(tables, jnp.float32)

    west_pack = pack_weights(moments[0][:, cols - 1], pieces[0][:, cols - 1], width)[:, None]
    from_west = from_prev(jnp.concatenate([tracer[:, cols - 3 :], west_pack], axis=1), "tile", True)
    from_east = from_next(tracer[:, :3], "tile", True)
    wide = jnp.concatenate([from_west[:, :3], tracer, from_east], axis=1)
    south_pack = jnp.pad(
        pack_weights(moments[1][rows - 1], pieces[1][rows - 1], width), ((3, 3), (0, 0))
    )[None]
    from_south = from_prev(jnp.concatenate([wide[rows - 3 :], south_pack], axis=0), "panel", False)
    from_north = from_next(wide[:3], "panel", False)
    padded = jnp.concatenate([from_south[:3], wide, from_north], axis=0)

    is_top = lax.axis_index("panel") == lax.axis_size("panel") - 1
    last_row = jnp.arange(rows) == rows - 1
    row_mask = jnp.where(jnp.logical_and(last_row, is_top), 0.0, 1.0).astype(jnp.float32)
    north_m = moments[1] * row_mask[:, None, None, None]
    zero_col = jnp.zeros_like(moments[0][:, :1])
    zero_row = jnp.zeros_like(moments[1][:1])
    face_m = jnp.stack(
        [
            jnp.concatenate([zero_col, moments[0][:, : cols - 1]], axis=1),
            moments[0],
            jnp.concatenate([zero_row, north_m[: rows - 1]], axis=0),
            north_m,
        ],
        axis=2,
    )
    face_p = jnp.stack(
        [
            jnp.concatenate([pieces[0][:, :1], pieces[0][:, : cols - 1]], axis=1),
            pieces[0],
            jnp.concatenate([pieces[1][:1], pieces[1][: rows - 1]], axis=0),
            pieces[1],
        ],
        axis=2,
    )
    weights = face_weights(face_m, face_p, tables)

    west_m, west_p = unpack_weights(from_west[:, 3], n_piece, n_moment)
    south_m, south_p = unpack_weights(from_south[3, 3 : 3 + cols], n_piece, n_moment)
    west_fix = face_weights(west_m[:, None], west_p[:, None], tables[:1])
    south_fix = face_weights(south_m[:, None], south_p[:, None], tables[2:3])
    weights = weights + jnp.pad(west_fix[:, None], ((0, 0), (0, cols - 1), (0, 0)))
    weights = weights + jnp.pad(south_fix[None], ((0, rows - 1), (0, 0), (0, 0)))
    weights = weights / cell_area[:, :, None]

    total = tracer.astype(jnp.float32)
    for tap, (dr, dc) in enumerate(offsets):
        piece = lax.slice(padded, (3 + dr, 3 + dc, 0), (3 + dr + rows, 3 + dc + cols, width))
        total = total + weights[:, :, tap][:, :, None] * piece.astype(jnp.float32)
    return total.astype(jnp.bfloat16)


def solution(mesh):
    in_specs = (
        P("panel", "tile", None),
        P(None, "panel", "tile", None, None),
        P(None, "panel", "tile", None),
        P("panel", "tile"),
    )
    out_specs = P("panel", "tile", None)
    return jax.shard_map(local, mesh=mesh, in_specs=in_specs, out_specs=out_specs, check_vma=False)
```

```python
import jax
import jax.numpy as jnp
import numpy as np
from jax import lax
from jax.sharding import PartitionSpec as P


def from_prev(value, axis, wrap):
    size = lax.axis_size(axis)
    pairs = [(i, (i + 1) % size) for i in range(size if wrap else size - 1)]
    return lax.ppermute(value, axis, pairs)


def from_next(value, axis, wrap):
    size = lax.axis_size(axis)
    pairs = [((i + 1) % size, i) for i in range(size if wrap else size - 1)]
    return lax.ppermute(value, axis, pairs)


def stencil_table():
    stencil = np.zeros((6, 3, 3))
    stencil[0, 1, 1] = 7.0 / 6.0
    stencil[0, 1, 0] = -1.0 / 24.0
    stencil[0, 1, 2] = -1.0 / 24.0
    stencil[0, 0, 1] = -1.0 / 24.0
    stencil[0, 2, 1] = -1.0 / 24.0
    stencil[1, 1, 2] = 0.5
    stencil[1, 1, 0] = -0.5
    stencil[2, 2, 1] = 0.5
    stencil[2, 0, 1] = -0.5
    stencil[3, 1, 2] = 0.5
    stencil[3, 1, 0] = 0.5
    stencil[3, 1, 1] = -1.0
    stencil[4, 2, 2] = 0.25
    stencil[4, 2, 0] = -0.25
    stencil[4, 0, 2] = -0.25
    stencil[4, 0, 0] = 0.25
    stencil[5, 2, 1] = 0.5
    stencil[5, 0, 1] = 0.5
    stencil[5, 1, 1] = -1.0
    return stencil


def face_tables():
    stencil = stencil_table()
    tables = np.zeros((4, 12, 6, 7, 7))
    for face, (direction, shift_row, shift_col, sign) in enumerate(
        ((0, 0, -1, 1.0), (0, 0, 0, -1.0), (1, -1, 0, 1.0), (1, 0, 0, -1.0))
    ):
        for code in range(12):
            if direction == 0:
                row_off, col_off = code // 4 - 1, code % 4 - 1
            else:
                row_off, col_off = code % 4 - 1, code // 4 - 1
            for inner_row in range(-1, 2):
                for inner_col in range(-1, 2):
                    r = row_off + inner_row + shift_row + 3
                    c = col_off + inner_col + shift_col + 3
                    tables[face, code, :, r, c] += sign * stencil[:, inner_row + 1, inner_col + 1]
    tables = tables.reshape(4, 12, 6, 49)
    used = np.nonzero(np.abs(tables).sum(axis=(0, 1, 2)) > 0)[0]
    return tables[..., used], [(int(t) // 7 - 3, int(t) % 7 - 3) for t in used]


def summed_moments(pieces, moments):
    codes = jnp.arange(12, dtype=jnp.int32)
    onehot = (pieces[..., None] == codes).astype(jnp.float32)
    return jnp.einsum("...ko,...km->...om", onehot, moments, precision=lax.Precision.HIGHEST)


def split3(value):
    hi = lax.reduce_precision(value, exponent_bits=8, mantissa_bits=7)
    rest = value - hi
    mid = lax.reduce_precision(rest, exponent_bits=8, mantissa_bits=7)
    lo = rest - mid
    return jnp.concatenate([hi, mid, lo], axis=-1).astype(jnp.bfloat16)


def join3(value, count):
    parts = [value[..., k * count : (k + 1) * count].astype(jnp.float32) for k in range(3)]
    return (parts[0] + parts[1]) + parts[2]


def pack_weights(moments, pieces, width):
    lead = moments.shape[:-2]
    flat = moments.reshape(lead + (moments.shape[-2] * moments.shape[-1],))
    packed = jnp.concatenate([split3(flat), pieces.astype(jnp.bfloat16)], axis=-1)
    return jnp.pad(packed, [(0, 0)] * len(lead) + [(0, width - packed.shape[-1])])


def unpack_weights(packed, n_piece, n_moment):
    count = n_piece * n_moment
    lead = packed.shape[:-1]
    moments = join3(packed[..., : 3 * count], count).reshape(lead + (n_piece, n_moment))
    pieces = packed[..., 3 * count : 3 * count + n_piece].astype(jnp.int32)
    return moments, pieces


def face_weights(moments, pieces, tables):
    n_code = tables.shape[1]
    onehot = (pieces[..., None] == jnp.arange(n_code, dtype=jnp.int32)).astype(jnp.float32)
    spread = jnp.sum(onehot[..., :, None] * moments[..., None, :], axis=-3)
    lead = spread.shape[:-3]
    flat = spread.reshape(lead + (-1,))
    return jnp.dot(flat, tables.reshape(-1, tables.shape[-1]), precision=lax.Precision.HIGHEST)


def tap_sum(weights, padded, row0, col0, nrow, ncol, offsets, taps):
    total = None
    for tap in taps:
        dr, dc = offsets[tap]
        piece = lax.slice(
            padded, (3 + row0 + dr, 3 + col0 + dc, 0), (3 + row0 + dr + nrow, 3 + col0 + dc + ncol, padded.shape[2])
        )
        term = weights[:, :, tap][:, :, None] * piece.astype(jnp.float32)
        total = term if total is None else total + term
    return total


def local(tracer, moments, pieces, cell_area):
    rows = tracer.shape[0]
    cols = tracer.shape[1]
    width = tracer.shape[2]
    n_piece = moments.shape[3]
    n_moment = moments.shape[4]
    np_tables, offsets = face_tables()
    tables = jnp.asarray(np_tables, jnp.float32)
    west_taps = [t for t in range(len(offsets)) if np.abs(np_tables[0, ..., t]).sum() > 0]
    south_taps = [t for t in range(len(offsets)) if np.abs(np_tables[2, ..., t]).sum() > 0]

    south_pack = pack_weights(moments[1][rows - 1], pieces[1][rows - 1], width)[None]
    from_south = from_prev(jnp.concatenate([tracer[rows - 3 :], south_pack], axis=0), "panel", False)
    from_north = from_next(tracer[:3], "panel", False)
    tall = jnp.concatenate([from_south[:3], tracer, from_north], axis=0)
    west_pack = jnp.pad(
        pack_weights(moments[0][:, cols - 1], pieces[0][:, cols - 1], width), ((3, 3), (0, 0))
    )[:, None]
    from_west = from_prev(jnp.concatenate([tall[:, cols - 3 :], west_pack], axis=1), "tile", True)
    from_east = from_next(tall[:, :3], "tile", True)
    padded = jnp.concatenate([from_west[:, :3], tall, from_east], axis=1)

    is_top = lax.axis_index("panel") == lax.axis_size("panel") - 1
    last_row = jnp.arange(rows) == rows - 1
    row_mask = jnp.where(jnp.logical_and(last_row, is_top), 0.0, 1.0).astype(jnp.float32)
    north_m = moments[1] * row_mask[:, None, None, None]
    zero_col = jnp.zeros_like(moments[0][:, :1])
    zero_row = jnp.zeros_like(moments[1][:1])
    face_m = jnp.stack(
        [
            jnp.concatenate([zero_col, moments[0][:, : cols - 1]], axis=1),
            moments[0],
            jnp.concatenate([zero_row, north_m[: rows - 1]], axis=0),
            north_m,
        ],
        axis=2,
    )
    face_p = jnp.stack(
        [
            jnp.concatenate([pieces[0][:, :1], pieces[0][:, : cols - 1]], axis=1),
            pieces[0],
            jnp.concatenate([pieces[1][:1], pieces[1][: rows - 1]], axis=0),
            pieces[1],
        ],
        axis=2,
    )
    weights = face_weights(face_m, face_p, tables) / cell_area[:, :, None]

    west_m, west_p = unpack_weights(from_west[3 : 3 + rows, 3], n_piece, n_moment)
    south_m, south_p = unpack_weights(from_south[3], n_piece, n_moment)
    west_fix = face_weights(west_m[:, None], west_p[:, None], tables[:1]) / cell_area[:, :1]
    south_fix = face_weights(south_m[:, None], south_p[:, None], tables[2:3]) / cell_area[0][:, None]

    total = tracer.astype(jnp.float32) + tap_sum(weights, padded, 0, 0, rows, cols, offsets, range(len(offsets)))
    west_add = tap_sum(west_fix[:, None], padded, 0, 0, rows, 1, offsets, west_taps)
    south_add = tap_sum(south_fix[None], padded, 0, 0, 1, cols, offsets, south_taps)
    total = total + jnp.pad(west_add, ((0, 0), (0, cols - 1), (0, 0)))
    total = total + jnp.pad(south_add, ((0, rows - 1), (0, 0), (0, 0)))
    return total.astype(jnp.bfloat16)


def solution(mesh):
    in_specs = (
        P("panel", "tile", None),
        P(None, "panel", "tile", None, None),
        P(None, "panel", "tile", None),
        P("panel", "tile"),
    )
    out_specs = P("panel", "tile", None)
    return jax.shard_map(local, mesh=mesh, in_specs=in_specs, out_specs=out_specs, check_vma=False)
```

```python
import functools
import math

import jax
import jax.numpy as jnp
import numpy as np
from jax import lax
from jax.experimental import pallas as pl
from jax.experimental.pallas import tpu as pltpu
from jax.sharding import PartitionSpec as P


INTERPRET = False


def from_prev(value, axis, wrap):
    size = lax.axis_size(axis)
    pairs = [(i, (i + 1) % size) for i in range(size if wrap else size - 1)]
    return lax.ppermute(value, axis, pairs)


def from_next(value, axis, wrap):
    size = lax.axis_size(axis)
    pairs = [((i + 1) % size, i) for i in range(size if wrap else size - 1)]
    return lax.ppermute(value, axis, pairs)


def stencil_table():
    stencil = np.zeros((6, 3, 3))
    stencil[0, 1, 1] = 7.0 / 6.0
    stencil[0, 1, 0] = -1.0 / 24.0
    stencil[0, 1, 2] = -1.0 / 24.0
    stencil[0, 0, 1] = -1.0 / 24.0
    stencil[0, 2, 1] = -1.0 / 24.0
    stencil[1, 1, 2] = 0.5
    stencil[1, 1, 0] = -0.5
    stencil[2, 2, 1] = 0.5
    stencil[2, 0, 1] = -0.5
    stencil[3, 1, 2] = 0.5
    stencil[3, 1, 0] = 0.5
    stencil[3, 1, 1] = -1.0
    stencil[4, 2, 2] = 0.25
    stencil[4, 2, 0] = -0.25
    stencil[4, 0, 2] = -0.25
    stencil[4, 0, 0] = 0.25
    stencil[5, 2, 1] = 0.5
    stencil[5, 0, 1] = 0.5
    stencil[5, 1, 1] = -1.0
    return stencil


def face_tables():
    stencil = stencil_table()
    tables = np.zeros((4, 12, 6, 7, 7))
    for face, (direction, shift_row, shift_col, sign) in enumerate(
        ((0, 0, -1, 1.0), (0, 0, 0, -1.0), (1, -1, 0, 1.0), (1, 0, 0, -1.0))
    ):
        for code in range(12):
            if direction == 0:
                row_off, col_off = code // 4 - 1, code % 4 - 1
            else:
                row_off, col_off = code % 4 - 1, code // 4 - 1
            for inner_row in range(-1, 2):
                for inner_col in range(-1, 2):
                    r = row_off + inner_row + shift_row + 3
                    c = col_off + inner_col + shift_col + 3
                    tables[face, code, :, r, c] += sign * stencil[:, inner_row + 1, inner_col + 1]
    tables = tables.reshape(4, 12, 6, 49)
    used = np.nonzero(np.abs(tables).sum(axis=(0, 1, 2)) > 0)[0]
    return tables[..., used], [(int(t) // 7 - 3, int(t) % 7 - 3) for t in used]


def summed_moments(pieces, moments):
    codes = jnp.arange(12, dtype=jnp.int32)
    onehot = (pieces[..., None] == codes).astype(jnp.float32)
    return jnp.einsum("...ko,...km->...om", onehot, moments, precision=lax.Precision.HIGHEST)


def split3(value):
    hi = lax.reduce_precision(value, exponent_bits=8, mantissa_bits=7)
    rest = value - hi
    mid = lax.reduce_precision(rest, exponent_bits=8, mantissa_bits=7)
    lo = rest - mid
    return jnp.concatenate([hi, mid, lo], axis=-1).astype(jnp.bfloat16)


def join3(value, count):
    parts = [value[..., k * count : (k + 1) * count].astype(jnp.float32) for k in range(3)]
    return (parts[0] + parts[1]) + parts[2]


def pack_weights(moments, pieces, width):
    lead = moments.shape[:-2]
    flat = moments.reshape(lead + (moments.shape[-2] * moments.shape[-1],))
    packed = jnp.concatenate([split3(flat), pieces.astype(jnp.bfloat16)], axis=-1)
    return jnp.pad(packed, [(0, 0)] * len(lead) + [(0, width - packed.shape[-1])])


def unpack_weights(packed, n_piece, n_moment):
    count = n_piece * n_moment
    lead = packed.shape[:-1]
    moments = join3(packed[..., : 3 * count], count).reshape(lead + (n_piece, n_moment))
    pieces = packed[..., 3 * count : 3 * count + n_piece].astype(jnp.int32)
    return moments, pieces


def face_weights(moments, pieces, tables):
    n_code = tables.shape[1]
    onehot = (pieces[..., None] == jnp.arange(n_code, dtype=jnp.int32)).astype(jnp.float32)
    spread = jnp.sum(onehot[..., :, None] * moments[..., None, :], axis=-3)
    lead = spread.shape[:-3]
    flat = spread.reshape(lead + (-1,))
    return jnp.dot(flat, tables.reshape(-1, tables.shape[-1]), precision=lax.Precision.HIGHEST)


def tap_sum(weights, padded, row0, col0, nrow, ncol, offsets, taps):
    total = None
    for tap in taps:
        dr, dc = offsets[tap]
        piece = lax.slice(
            padded, (3 + row0 + dr, 3 + col0 + dc, 0), (3 + row0 + dr + nrow, 3 + col0 + dc + ncol, padded.shape[2])
        )
        term = weights[:, :, tap][:, :, None] * piece.astype(jnp.float32)
        total = term if total is None else total + term
    return total


def tap_kernel(offsets, chunk, w_ref, p_ref, t_ref, o_ref, s_ref):
    s_ref[...] = p_ref[...].astype(jnp.float32)
    rows, cols, width = t_ref.shape

    def row(i, carry):
        for start in range(0, width, chunk):
            lanes = pl.ds(start, chunk)
            acc = t_ref[i, :, lanes].astype(jnp.float32)
            for tap, (dr, dc) in enumerate(offsets):
                w = w_ref[i, :, tap : tap + 1]
                acc = acc + w * s_ref[i + 3 + dr, pl.ds(3 + dc, cols), lanes]
            o_ref[i, :, lanes] = acc.astype(o_ref.dtype)
        return carry

    lax.fori_loop(0, rows, row, 0)


def apply_taps(weights, padded, tracer, offsets):
    return pl.pallas_call(
        functools.partial(tap_kernel, offsets, math.gcd(tracer.shape[2], 384)),
        out_shape=jax.ShapeDtypeStruct(tracer.shape, jnp.bfloat16),
        scratch_shapes=[pltpu.VMEM(padded.shape, jnp.float32)],
        interpret=INTERPRET,
    )(weights, padded, tracer)


def local(tracer, moments, pieces, cell_area):
    rows = tracer.shape[0]
    cols = tracer.shape[1]
    width = tracer.shape[2]
    n_piece = moments.shape[3]
    n_moment = moments.shape[4]
    np_tables, offsets = face_tables()
    tables = jnp.asarray(np_tables, jnp.float32)
    west_taps = [t for t in range(len(offsets)) if np.abs(np_tables[0, ..., t]).sum() > 0]
    south_taps = [t for t in range(len(offsets)) if np.abs(np_tables[2, ..., t]).sum() > 0]

    south_pack = pack_weights(moments[1][rows - 1], pieces[1][rows - 1], width)[None]
    from_south = from_prev(jnp.concatenate([tracer[rows - 3 :], south_pack], axis=0), "panel", False)
    from_north = from_next(tracer[:3], "panel", False)
    tall = jnp.concatenate([from_south[:3], tracer, from_north], axis=0)
    west_pack = jnp.pad(
        pack_weights(moments[0][:, cols - 1], pieces[0][:, cols - 1], width), ((3, 3), (0, 0))
    )[:, None]
    from_west = from_prev(jnp.concatenate([tall[:, cols - 3 :], west_pack], axis=1), "tile", True)
    from_east = from_next(tall[:, :3], "tile", True)
    padded = jnp.concatenate([from_west[:, :3], tall, from_east], axis=1)

    is_top = lax.axis_index("panel") == lax.axis_size("panel") - 1
    last_row = jnp.arange(rows) == rows - 1
    row_mask = jnp.where(jnp.logical_and(last_row, is_top), 0.0, 1.0).astype(jnp.float32)
    north_m = moments[1] * row_mask[:, None, None, None]
    zero_col = jnp.zeros_like(moments[0][:, :1])
    zero_row = jnp.zeros_like(moments[1][:1])
    face_m = jnp.stack(
        [
            jnp.concatenate([zero_col, moments[0][:, : cols - 1]], axis=1),
            moments[0],
            jnp.concatenate([zero_row, north_m[: rows - 1]], axis=0),
            north_m,
        ],
        axis=2,
    )
    face_p = jnp.stack(
        [
            jnp.concatenate([pieces[0][:, :1], pieces[0][:, : cols - 1]], axis=1),
            pieces[0],
            jnp.concatenate([pieces[1][:1], pieces[1][: rows - 1]], axis=0),
            pieces[1],
        ],
        axis=2,
    )
    weights = face_weights(face_m, face_p, tables)
    weights = lax.optimization_barrier(weights)

    west_m, west_p = unpack_weights(from_west[3 : 3 + rows, 3], n_piece, n_moment)
    south_m, south_p = unpack_weights(from_south[3], n_piece, n_moment)
    west_fix = face_weights(west_m[:, None], west_p[:, None], tables[:1])
    south_fix = face_weights(south_m[:, None], south_p[:, None], tables[2:3])
    weights = weights + jnp.pad(west_fix[:, None], ((0, 0), (0, cols - 1), (0, 0)))
    weights = weights + jnp.pad(south_fix[None], ((0, rows - 1), (0, 0), (0, 0)))
    weights = weights / cell_area[:, :, None]
    return apply_taps(weights, padded, tracer, offsets)


def solution(mesh):
    in_specs = (
        P("panel", "tile", None),
        P(None, "panel", "tile", None, None),
        P(None, "panel", "tile", None),
        P("panel", "tile"),
    )
    out_specs = P("panel", "tile", None)
    return jax.shard_map(local, mesh=mesh, in_specs=in_specs, out_specs=out_specs, check_vma=False)
```

```python
import functools
import math

import jax
import jax.numpy as jnp
import numpy as np
from jax import lax
from jax.experimental import pallas as pl
from jax.experimental.pallas import tpu as pltpu
from jax.sharding import PartitionSpec as P


INTERPRET = False


def from_prev(value, axis, wrap):
    size = lax.axis_size(axis)
    pairs = [(i, (i + 1) % size) for i in range(size if wrap else size - 1)]
    return lax.ppermute(value, axis, pairs)


def from_next(value, axis, wrap):
    size = lax.axis_size(axis)
    pairs = [((i + 1) % size, i) for i in range(size if wrap else size - 1)]
    return lax.ppermute(value, axis, pairs)


def stencil_table():
    stencil = np.zeros((6, 3, 3))
    stencil[0, 1, 1] = 7.0 / 6.0
    stencil[0, 1, 0] = -1.0 / 24.0
    stencil[0, 1, 2] = -1.0 / 24.0
    stencil[0, 0, 1] = -1.0 / 24.0
    stencil[0, 2, 1] = -1.0 / 24.0
    stencil[1, 1, 2] = 0.5
    stencil[1, 1, 0] = -0.5
    stencil[2, 2, 1] = 0.5
    stencil[2, 0, 1] = -0.5
    stencil[3, 1, 2] = 0.5
    stencil[3, 1, 0] = 0.5
    stencil[3, 1, 1] = -1.0
    stencil[4, 2, 2] = 0.25
    stencil[4, 2, 0] = -0.25
    stencil[4, 0, 2] = -0.25
    stencil[4, 0, 0] = 0.25
    stencil[5, 2, 1] = 0.5
    stencil[5, 0, 1] = 0.5
    stencil[5, 1, 1] = -1.0
    return stencil


def face_tables():
    stencil = stencil_table()
    tables = np.zeros((4, 12, 6, 7, 7))
    for face, (direction, shift_row, shift_col, sign) in enumerate(
        ((0, 0, -1, 1.0), (0, 0, 0, -1.0), (1, -1, 0, 1.0), (1, 0, 0, -1.0))
    ):
        for code in range(12):
            if direction == 0:
                row_off, col_off = code // 4 - 1, code % 4 - 1
            else:
                row_off, col_off = code % 4 - 1, code // 4 - 1
            for inner_row in range(-1, 2):
                for inner_col in range(-1, 2):
                    r = row_off + inner_row + shift_row + 3
                    c = col_off + inner_col + shift_col + 3
                    tables[face, code, :, r, c] += sign * stencil[:, inner_row + 1, inner_col + 1]
    tables = tables.reshape(4, 12, 6, 49)
    used = np.nonzero(np.abs(tables).sum(axis=(0, 1, 2)) > 0)[0]
    return tables[..., used], [(int(t) // 7 - 3, int(t) % 7 - 3) for t in used]


def summed_moments(pieces, moments):
    codes = jnp.arange(12, dtype=jnp.int32)
    onehot = (pieces[..., None] == codes).astype(jnp.float32)
    return jnp.einsum("...ko,...km->...om", onehot, moments, precision=lax.Precision.HIGHEST)


def split3(value):
    hi = lax.reduce_precision(value, exponent_bits=8, mantissa_bits=7)
    rest = value - hi
    mid = lax.reduce_precision(rest, exponent_bits=8, mantissa_bits=7)
    lo = rest - mid
    return jnp.concatenate([hi, mid, lo], axis=-1).astype(jnp.bfloat16)


def join3(value, count):
    parts = [value[..., k * count : (k + 1) * count].astype(jnp.float32) for k in range(3)]
    return (parts[0] + parts[1]) + parts[2]


def pack_weights(moments, pieces, width):
    lead = moments.shape[:-2]
    flat = moments.reshape(lead + (moments.shape[-2] * moments.shape[-1],))
    packed = jnp.concatenate([split3(flat), pieces.astype(jnp.bfloat16)], axis=-1)
    return jnp.pad(packed, [(0, 0)] * len(lead) + [(0, width - packed.shape[-1])])


def unpack_weights(packed, n_piece, n_moment):
    count = n_piece * n_moment
    lead = packed.shape[:-1]
    moments = join3(packed[..., : 3 * count], count).reshape(lead + (n_piece, n_moment))
    pieces = packed[..., 3 * count : 3 * count + n_piece].astype(jnp.int32)
    return moments, pieces


def face_weights(moments, pieces, tables):
    n_code = tables.shape[1]
    onehot = (pieces[..., None] == jnp.arange(n_code, dtype=jnp.int32)).astype(jnp.float32)
    spread = jnp.sum(onehot[..., :, None] * moments[..., None, :], axis=-3)
    lead = spread.shape[:-3]
    flat = spread.reshape(lead + (-1,))
    return jnp.dot(flat, tables.reshape(-1, tables.shape[-1]), precision=lax.Precision.HIGHEST)


def tap_sum(weights, padded, row0, col0, nrow, ncol, offsets, taps):
    total = None
    for tap in taps:
        dr, dc = offsets[tap]
        piece = lax.slice(
            padded, (3 + row0 + dr, 3 + col0 + dc, 0), (3 + row0 + dr + nrow, 3 + col0 + dc + ncol, padded.shape[2])
        )
        term = weights[:, :, tap][:, :, None] * piece.astype(jnp.float32)
        total = term if total is None else total + term
    return total


def tap_kernel(offsets, chunk, w_ref, south_ref, t_ref, north_ref, west_ref, east_ref, o_ref, s_ref, sh_ref):
    rows, cols, width = t_ref.shape
    halo = south_ref.shape[0] - 1
    f32 = jnp.float32
    s_ref[0:halo, halo : halo + cols] = south_ref[0:halo].astype(f32)
    s_ref[halo : halo + rows, halo : halo + cols] = t_ref[...].astype(f32)
    s_ref[halo + rows :, halo : halo + cols] = north_ref[...].astype(f32)
    s_ref[:, 0:halo] = west_ref[:, 0:halo].astype(f32)
    s_ref[:, halo + cols :] = east_ref[...].astype(f32)
    for shift in range(2 * halo + 1):
        sh_ref[shift] = s_ref[:, pl.ds(shift, cols), :]

    def row(i, carry):
        for start in range(0, width, chunk):
            lanes = pl.ds(start, chunk)
            acc = s_ref[i + halo, pl.ds(halo, cols), lanes]
            for tap, (dr, dc) in enumerate(offsets):
                w = w_ref[i, :, tap : tap + 1]
                acc = acc + w * sh_ref[dc + halo, i + halo + dr, :, lanes]
            o_ref[i, :, lanes] = acc.astype(o_ref.dtype)
        return carry

    lax.fori_loop(0, rows, row, 0)


def apply_taps(weights, from_south, tracer, from_north, from_west, from_east, offsets):
    rows, cols, width = tracer.shape
    halo = from_north.shape[0]
    return pl.pallas_call(
        functools.partial(tap_kernel, offsets, math.gcd(width, 384)),
        out_shape=jax.ShapeDtypeStruct(tracer.shape, jnp.bfloat16),
        scratch_shapes=[
            pltpu.VMEM((rows + 2 * halo, cols + 2 * halo, width), jnp.float32),
            pltpu.VMEM((2 * halo + 1, rows + 2 * halo, cols, width), jnp.float32),
        ],
        interpret=INTERPRET,
    )(weights, from_south, tracer, from_north, from_west, from_east)


def local(tracer, moments, pieces, cell_area):
    rows = tracer.shape[0]
    cols = tracer.shape[1]
    width = tracer.shape[2]
    n_piece = moments.shape[3]
    n_moment = moments.shape[4]
    np_tables, offsets = face_tables()
    tables = jnp.asarray(np_tables, jnp.float32)
    west_taps = [t for t in range(len(offsets)) if np.abs(np_tables[0, ..., t]).sum() > 0]
    south_taps = [t for t in range(len(offsets)) if np.abs(np_tables[2, ..., t]).sum() > 0]

    south_pack = pack_weights(moments[1][rows - 1], pieces[1][rows - 1], width)[None]
    from_south = from_prev(jnp.concatenate([tracer[rows - 3 :], south_pack], axis=0), "panel", False)
    from_north = from_next(tracer[:3], "panel", False)
    tall = jnp.concatenate([from_south[:3], tracer, from_north], axis=0)
    west_pack = jnp.pad(
        pack_weights(moments[0][:, cols - 1], pieces[0][:, cols - 1], width), ((3, 3), (0, 0))
    )[:, None]
    from_west = from_prev(jnp.concatenate([tall[:, cols - 3 :], west_pack], axis=1), "tile", True)
    from_east = from_next(tall[:, :3], "tile", True)

    is_top = lax.axis_index("panel") == lax.axis_size("panel") - 1
    last_row = jnp.arange(rows) == rows - 1
    row_mask = jnp.where(jnp.logical_and(last_row, is_top), 0.0, 1.0).astype(jnp.float32)
    north_m = moments[1] * row_mask[:, None, None, None]
    zero_col = jnp.zeros_like(moments[0][:, :1])
    zero_row = jnp.zeros_like(moments[1][:1])
    face_m = jnp.stack(
        [
            jnp.concatenate([zero_col, moments[0][:, : cols - 1]], axis=1),
            moments[0],
            jnp.concatenate([zero_row, north_m[: rows - 1]], axis=0),
            north_m,
        ],
        axis=2,
    )
    face_p = jnp.stack(
        [
            jnp.concatenate([pieces[0][:, :1], pieces[0][:, : cols - 1]], axis=1),
            pieces[0],
            jnp.concatenate([pieces[1][:1], pieces[1][: rows - 1]], axis=0),
            pieces[1],
        ],
        axis=2,
    )
    weights = face_weights(face_m, face_p, tables)
    weights = lax.optimization_barrier(weights)

    west_m, west_p = unpack_weights(from_west[3 : 3 + rows, 3], n_piece, n_moment)
    south_m, south_p = unpack_weights(from_south[3], n_piece, n_moment)
    west_fix = face_weights(west_m[:, None], west_p[:, None], tables[:1])
    south_fix = face_weights(south_m[:, None], south_p[:, None], tables[2:3])
    weights = weights + jnp.pad(west_fix[:, None], ((0, 0), (0, cols - 1), (0, 0)))
    weights = weights + jnp.pad(south_fix[None], ((0, rows - 1), (0, 0), (0, 0)))
    weights = weights / cell_area[:, :, None]
    return apply_taps(weights, from_south, tracer, from_north, from_west, from_east, offsets)


def solution(mesh):
    in_specs = (
        P("panel", "tile", None),
        P(None, "panel", "tile", None, None),
        P(None, "panel", "tile", None),
        P("panel", "tile"),
    )
    out_specs = P("panel", "tile", None)
    return jax.shard_map(local, mesh=mesh, in_specs=in_specs, out_specs=out_specs, check_vma=False)
```

```python
import functools
import math

import jax
import jax.numpy as jnp
import numpy as np
from jax import lax
from jax.experimental import pallas as pl
from jax.experimental.pallas import tpu as pltpu
from jax.sharding import PartitionSpec as P


INTERPRET = False


def from_prev(value, axis, wrap):
    size = lax.axis_size(axis)
    pairs = [(i, (i + 1) % size) for i in range(size if wrap else size - 1)]
    return lax.ppermute(value, axis, pairs)


def from_next(value, axis, wrap):
    size = lax.axis_size(axis)
    pairs = [((i + 1) % size, i) for i in range(size if wrap else size - 1)]
    return lax.ppermute(value, axis, pairs)


def stencil_table():
    stencil = np.zeros((6, 3, 3))
    stencil[0, 1, 1] = 7.0 / 6.0
    stencil[0, 1, 0] = -1.0 / 24.0
    stencil[0, 1, 2] = -1.0 / 24.0
    stencil[0, 0, 1] = -1.0 / 24.0
    stencil[0, 2, 1] = -1.0 / 24.0
    stencil[1, 1, 2] = 0.5
    stencil[1, 1, 0] = -0.5
    stencil[2, 2, 1] = 0.5
    stencil[2, 0, 1] = -0.5
    stencil[3, 1, 2] = 0.5
    stencil[3, 1, 0] = 0.5
    stencil[3, 1, 1] = -1.0
    stencil[4, 2, 2] = 0.25
    stencil[4, 2, 0] = -0.25
    stencil[4, 0, 2] = -0.25
    stencil[4, 0, 0] = 0.25
    stencil[5, 2, 1] = 0.5
    stencil[5, 0, 1] = 0.5
    stencil[5, 1, 1] = -1.0
    return stencil


def face_tables():
    stencil = stencil_table()
    tables = np.zeros((4, 12, 6, 7, 7))
    for face, (direction, shift_row, shift_col, sign) in enumerate(
        ((0, 0, -1, 1.0), (0, 0, 0, -1.0), (1, -1, 0, 1.0), (1, 0, 0, -1.0))
    ):
        for code in range(12):
            if direction == 0:
                row_off, col_off = code // 4 - 1, code % 4 - 1
            else:
                row_off, col_off = code % 4 - 1, code // 4 - 1
            for inner_row in range(-1, 2):
                for inner_col in range(-1, 2):
                    r = row_off + inner_row + shift_row + 3
                    c = col_off + inner_col + shift_col + 3
                    tables[face, code, :, r, c] += sign * stencil[:, inner_row + 1, inner_col + 1]
    tables = tables.reshape(4, 12, 6, 49)
    used = np.nonzero(np.abs(tables).sum(axis=(0, 1, 2)) > 0)[0]
    return tables[..., used], [(int(t) // 7 - 3, int(t) % 7 - 3) for t in used]


def summed_moments(pieces, moments):
    codes = jnp.arange(12, dtype=jnp.int32)
    onehot = (pieces[..., None] == codes).astype(jnp.float32)
    return jnp.einsum("...ko,...km->...om", onehot, moments, precision=lax.Precision.HIGHEST)


def split3(value):
    hi = lax.reduce_precision(value, exponent_bits=8, mantissa_bits=7)
    rest = value - hi
    mid = lax.reduce_precision(rest, exponent_bits=8, mantissa_bits=7)
    lo = rest - mid
    return jnp.concatenate([hi, mid, lo], axis=-1).astype(jnp.bfloat16)


def join3(value, count):
    parts = [value[..., k * count : (k + 1) * count].astype(jnp.float32) for k in range(3)]
    return (parts[0] + parts[1]) + parts[2]


def pack_weights(moments, pieces, width):
    lead = moments.shape[:-2]
    flat = moments.reshape(lead + (moments.shape[-2] * moments.shape[-1],))
    packed = jnp.concatenate([split3(flat), pieces.astype(jnp.bfloat16)], axis=-1)
    return jnp.pad(packed, [(0, 0)] * len(lead) + [(0, width - packed.shape[-1])])


def unpack_weights(packed, n_piece, n_moment):
    count = n_piece * n_moment
    lead = packed.shape[:-1]
    moments = join3(packed[..., : 3 * count], count).reshape(lead + (n_piece, n_moment))
    pieces = packed[..., 3 * count : 3 * count + n_piece].astype(jnp.int32)
    return moments, pieces


def face_weights(moments, pieces, tables):
    n_code = tables.shape[1]
    onehot = (pieces[..., None] == jnp.arange(n_code, dtype=jnp.int32)).astype(jnp.float32)
    spread = jnp.sum(onehot[..., :, None] * moments[..., None, :], axis=-3)
    lead = spread.shape[:-3]
    flat = spread.reshape(lead + (-1,))
    return jnp.dot(flat, tables.reshape(-1, tables.shape[-1]), precision=lax.Precision.HIGHEST)


def tap_sum(weights, padded, row0, col0, nrow, ncol, offsets, taps):
    total = None
    for tap in taps:
        dr, dc = offsets[tap]
        piece = lax.slice(
            padded, (3 + row0 + dr, 3 + col0 + dc, 0), (3 + row0 + dr + nrow, 3 + col0 + dc + ncol, padded.shape[2])
        )
        term = weights[:, :, tap][:, :, None] * piece.astype(jnp.float32)
        total = term if total is None else total + term
    return total


def face_weights_t(moments, pieces, tables):
    n_row, n_col = moments.shape[:2]
    n_code = tables.shape[1]
    m_t = jnp.transpose(moments, (2, 3, 4, 0, 1)).reshape(moments.shape[2:] + (n_row * n_col,))
    p_t = jnp.transpose(pieces, (2, 3, 0, 1)).reshape(pieces.shape[2:] + (n_row * n_col,))
    onehot = (p_t[:, :, None, :] == jnp.arange(n_code, dtype=jnp.int32)[None, None, :, None]).astype(jnp.float32)
    spread = jnp.sum(onehot[:, :, :, None, :] * m_t[:, :, None, :, :], axis=1)
    flat = spread.reshape(-1, n_row * n_col)
    table_t = tables.reshape(-1, tables.shape[-1]).T
    w_t = jnp.dot(table_t, flat, precision=lax.Precision.HIGHEST)
    return w_t.T.reshape(n_row, n_col, tables.shape[-1])


def tap_kernel(offsets, chunk, w_ref, p_ref, t_ref, o_ref, s_ref):
    s_ref[...] = p_ref[...].astype(jnp.float32)
    rows, cols, width = t_ref.shape

    def row(i, carry):
        for start in range(0, width, chunk):
            lanes = pl.ds(start, chunk)
            acc = t_ref[i, :, lanes].astype(jnp.float32)
            for tap, (dr, dc) in enumerate(offsets):
                w = w_ref[i, :, tap : tap + 1]
                acc = acc + w * s_ref[i + 3 + dr, pl.ds(3 + dc, cols), lanes]
            o_ref[i, :, lanes] = acc.astype(o_ref.dtype)
        return carry

    lax.fori_loop(0, rows, row, 0)


def apply_taps(weights, padded, tracer, offsets):
    return pl.pallas_call(
        functools.partial(tap_kernel, offsets, math.gcd(tracer.shape[2], 384)),
        out_shape=jax.ShapeDtypeStruct(tracer.shape, jnp.bfloat16),
        scratch_shapes=[pltpu.VMEM(padded.shape, jnp.float32)],
        interpret=INTERPRET,
    )(weights, padded, tracer)


def local(tracer, moments, pieces, cell_area):
    rows = tracer.shape[0]
    cols = tracer.shape[1]
    width = tracer.shape[2]
    n_piece = moments.shape[3]
    n_moment = moments.shape[4]
    np_tables, offsets = face_tables()
    tables = jnp.asarray(np_tables, jnp.float32)
    west_taps = [t for t in range(len(offsets)) if np.abs(np_tables[0, ..., t]).sum() > 0]
    south_taps = [t for t in range(len(offsets)) if np.abs(np_tables[2, ..., t]).sum() > 0]

    south_pack = pack_weights(moments[1][rows - 1], pieces[1][rows - 1], width)[None]
    from_south = from_prev(jnp.concatenate([tracer[rows - 3 :], south_pack], axis=0), "panel", False)
    from_north = from_next(tracer[:3], "panel", False)
    tall = jnp.concatenate([from_south[:3], tracer, from_north], axis=0)
    west_pack = jnp.pad(
        pack_weights(moments[0][:, cols - 1], pieces[0][:, cols - 1], width), ((3, 3), (0, 0))
    )[:, None]
    from_west = from_prev(jnp.concatenate([tall[:, cols - 3 :], west_pack], axis=1), "tile", True)
    from_east = from_next(tall[:, :3], "tile", True)
    padded = jnp.concatenate([from_west[:, :3], tall, from_east], axis=1)

    is_top = lax.axis_index("panel") == lax.axis_size("panel") - 1
    last_row = jnp.arange(rows) == rows - 1
    row_mask = jnp.where(jnp.logical_and(last_row, is_top), 0.0, 1.0).astype(jnp.float32)
    north_m = moments[1] * row_mask[:, None, None, None]
    zero_col = jnp.zeros_like(moments[0][:, :1])
    zero_row = jnp.zeros_like(moments[1][:1])
    face_m = jnp.stack(
        [
            jnp.concatenate([zero_col, moments[0][:, : cols - 1]], axis=1),
            moments[0],
            jnp.concatenate([zero_row, north_m[: rows - 1]], axis=0),
            north_m,
        ],
        axis=2,
    )
    face_p = jnp.stack(
        [
            jnp.concatenate([pieces[0][:, :1], pieces[0][:, : cols - 1]], axis=1),
            pieces[0],
            jnp.concatenate([pieces[1][:1], pieces[1][: rows - 1]], axis=0),
            pieces[1],
        ],
        axis=2,
    )
    weights = face_weights_t(face_m, face_p, tables)
    weights = lax.optimization_barrier(weights)

    west_m, west_p = unpack_weights(from_west[3 : 3 + rows, 3], n_piece, n_moment)
    south_m, south_p = unpack_weights(from_south[3], n_piece, n_moment)
    west_fix = face_weights(west_m[:, None], west_p[:, None], tables[:1])
    south_fix = face_weights(south_m[:, None], south_p[:, None], tables[2:3])
    weights = weights + jnp.pad(west_fix[:, None], ((0, 0), (0, cols - 1), (0, 0)))
    weights = weights + jnp.pad(south_fix[None], ((0, rows - 1), (0, 0), (0, 0)))
    weights = weights / cell_area[:, :, None]
    return apply_taps(weights, padded, tracer, offsets)


def solution(mesh):
    in_specs = (
        P("panel", "tile", None),
        P(None, "panel", "tile", None, None),
        P(None, "panel", "tile", None),
        P("panel", "tile"),
    )
    out_specs = P("panel", "tile", None)
    return jax.shard_map(local, mesh=mesh, in_specs=in_specs, out_specs=out_specs, check_vma=False)
```

```python
import functools
import math

import jax
import jax.numpy as jnp
import numpy as np
from jax import lax
from jax.experimental import pallas as pl
from jax.experimental.pallas import tpu as pltpu
from jax.sharding import PartitionSpec as P


INTERPRET = False


def from_prev(value, axis, wrap):
    size = lax.axis_size(axis)
    pairs = [(i, (i + 1) % size) for i in range(size if wrap else size - 1)]
    return lax.ppermute(value, axis, pairs)


def from_next(value, axis, wrap):
    size = lax.axis_size(axis)
    pairs = [((i + 1) % size, i) for i in range(size if wrap else size - 1)]
    return lax.ppermute(value, axis, pairs)


def stencil_table():
    stencil = np.zeros((6, 3, 3))
    stencil[0, 1, 1] = 7.0 / 6.0
    stencil[0, 1, 0] = -1.0 / 24.0
    stencil[0, 1, 2] = -1.0 / 24.0
    stencil[0, 0, 1] = -1.0 / 24.0
    stencil[0, 2, 1] = -1.0 / 24.0
    stencil[1, 1, 2] = 0.5
    stencil[1, 1, 0] = -0.5
    stencil[2, 2, 1] = 0.5
    stencil[2, 0, 1] = -0.5
    stencil[3, 1, 2] = 0.5
    stencil[3, 1, 0] = 0.5
    stencil[3, 1, 1] = -1.0
    stencil[4, 2, 2] = 0.25
    stencil[4, 2, 0] = -0.25
    stencil[4, 0, 2] = -0.25
    stencil[4, 0, 0] = 0.25
    stencil[5, 2, 1] = 0.5
    stencil[5, 0, 1] = 0.5
    stencil[5, 1, 1] = -1.0
    return stencil


def face_tables():
    stencil = stencil_table()
    tables = np.zeros((4, 12, 6, 7, 7))
    for face, (direction, shift_row, shift_col, sign) in enumerate(
        ((0, 0, -1, 1.0), (0, 0, 0, -1.0), (1, -1, 0, 1.0), (1, 0, 0, -1.0))
    ):
        for code in range(12):
            if direction == 0:
                row_off, col_off = code // 4 - 1, code % 4 - 1
            else:
                row_off, col_off = code % 4 - 1, code // 4 - 1
            for inner_row in range(-1, 2):
                for inner_col in range(-1, 2):
                    r = row_off + inner_row + shift_row + 3
                    c = col_off + inner_col + shift_col + 3
                    tables[face, code, :, r, c] += sign * stencil[:, inner_row + 1, inner_col + 1]
    tables = tables.reshape(4, 12, 6, 49)
    used = np.nonzero(np.abs(tables).sum(axis=(0, 1, 2)) > 0)[0]
    return tables[..., used], [(int(t) // 7 - 3, int(t) % 7 - 3) for t in used], tables


def summed_moments(pieces, moments):
    codes = jnp.arange(12, dtype=jnp.int32)
    onehot = (pieces[..., None] == codes).astype(jnp.float32)
    return jnp.einsum("...ko,...km->...om", onehot, moments, precision=lax.Precision.HIGHEST)


def split3(value):
    hi = lax.reduce_precision(value, exponent_bits=8, mantissa_bits=7)
    rest = value - hi
    mid = lax.reduce_precision(rest, exponent_bits=8, mantissa_bits=7)
    lo = rest - mid
    return jnp.concatenate([hi, mid, lo], axis=-1).astype(jnp.bfloat16)


def join3(value, count):
    parts = [value[..., k * count : (k + 1) * count].astype(jnp.float32) for k in range(3)]
    return (parts[0] + parts[1]) + parts[2]


def pack_weights(moments, pieces, width):
    lead = moments.shape[:-2]
    flat = moments.reshape(lead + (moments.shape[-2] * moments.shape[-1],))
    packed = jnp.concatenate([split3(flat), pieces.astype(jnp.bfloat16)], axis=-1)
    return jnp.pad(packed, [(0, 0)] * len(lead) + [(0, width - packed.shape[-1])])


def unpack_weights(packed, n_piece, n_moment):
    count = n_piece * n_moment
    lead = packed.shape[:-1]
    moments = join3(packed[..., : 3 * count], count).reshape(lead + (n_piece, n_moment))
    pieces = packed[..., 3 * count : 3 * count + n_piece].astype(jnp.int32)
    return moments, pieces


def face_weights(moments, pieces, tables):
    n_code = tables.shape[1]
    onehot = (pieces[..., None] == jnp.arange(n_code, dtype=jnp.int32)).astype(jnp.float32)
    spread = jnp.sum(onehot[..., :, None] * moments[..., None, :], axis=-3)
    lead = spread.shape[:-3]
    flat = spread.reshape(lead + (-1,))
    return jnp.dot(flat, tables.reshape(-1, tables.shape[-1]), precision=lax.Precision.HIGHEST)


def tap_sum(weights, padded, row0, col0, nrow, ncol, offsets, taps):
    total = None
    for tap in taps:
        dr, dc = offsets[tap]
        piece = lax.slice(
            padded, (3 + row0 + dr, 3 + col0 + dc, 0), (3 + row0 + dr + nrow, 3 + col0 + dc + ncol, padded.shape[2])
        )
        term = weights[:, :, tap][:, :, None] * piece.astype(jnp.float32)
        total = term if total is None else total + term
    return total


def tap_kernel(offsets, chunk, w_ref, p_ref, t_ref, o_ref, s_ref):
    s_ref[...] = p_ref[...].astype(jnp.float32)
    rows, cols, width = t_ref.shape

    def row(i, carry):
        for start in range(0, width, chunk):
            lanes = pl.ds(start, chunk)
            acc = t_ref[i, :, lanes].astype(jnp.float32)
            for tap, (dr, dc) in enumerate(offsets):
                w = w_ref[i, :, tap : tap + 1]
                acc = acc + w * s_ref[i + 3 + dr, pl.ds(3 + dc, cols), lanes]
            o_ref[i, :, lanes] = acc.astype(o_ref.dtype)
        return carry

    lax.fori_loop(0, rows, row, 0)


def apply_taps(weights, padded, tracer, offsets):
    return pl.pallas_call(
        functools.partial(tap_kernel, offsets, math.gcd(tracer.shape[2], 384)),
        out_shape=jax.ShapeDtypeStruct(tracer.shape, jnp.bfloat16),
        scratch_shapes=[pltpu.VMEM(padded.shape, jnp.float32)],
        interpret=INTERPRET,
    )(weights, padded, tracer)


def local(tracer, moments, pieces, cell_area):
    rows = tracer.shape[0]
    cols = tracer.shape[1]
    width = tracer.shape[2]
    n_piece = moments.shape[3]
    n_moment = moments.shape[4]
    _, _, np_full = face_tables()
    tables_full = jnp.asarray(np_full, jnp.float32)

    south_pack = pack_weights(moments[1][rows - 1], pieces[1][rows - 1], width)[None]
    from_south = from_prev(jnp.concatenate([tracer[rows - 3 :], south_pack], axis=0), "panel", False)
    from_north = from_next(tracer[:3], "panel", False)
    tall = jnp.concatenate([from_south[:3], tracer, from_north], axis=0)
    west_pack = jnp.pad(
        pack_weights(moments[0][:, cols - 1], pieces[0][:, cols - 1], width), ((3, 3), (0, 0))
    )[:, None]
    from_west = from_prev(jnp.concatenate([tall[:, cols - 3 :], west_pack], axis=1), "tile", True)
    from_east = from_next(tall[:, :3], "tile", True)
    padded = jnp.concatenate([from_west[:, :3], tall, from_east], axis=1)

    is_top = lax.axis_index("panel") == lax.axis_size("panel") - 1
    last_row = jnp.arange(rows) == rows - 1
    row_mask = jnp.where(jnp.logical_and(last_row, is_top), 0.0, 1.0).astype(jnp.float32)
    north_m = moments[1] * row_mask[:, None, None, None]
    zero_col = jnp.zeros_like(moments[0][:, :1])
    zero_row = jnp.zeros_like(moments[1][:1])
    face_m = jnp.stack(
        [
            jnp.concatenate([zero_col, moments[0][:, : cols - 1]], axis=1),
            moments[0],
            jnp.concatenate([zero_row, north_m[: rows - 1]], axis=0),
            north_m,
        ],
        axis=2,
    )
    face_p = jnp.stack(
        [
            jnp.concatenate([pieces[0][:, :1], pieces[0][:, : cols - 1]], axis=1),
            pieces[0],
            jnp.concatenate([pieces[1][:1], pieces[1][: rows - 1]], axis=0),
            pieces[1],
        ],
        axis=2,
    )
    weights = face_weights(face_m, face_p, tables_full)
    weights = lax.optimization_barrier(weights)

    west_m, west_p = unpack_weights(from_west[3 : 3 + rows, 3], n_piece, n_moment)
    south_m, south_p = unpack_weights(from_south[3], n_piece, n_moment)
    west_fix = face_weights(west_m[:, None], west_p[:, None], tables_full[:1])
    south_fix = face_weights(south_m[:, None], south_p[:, None], tables_full[2:3])
    weights = weights + jnp.pad(west_fix[:, None], ((0, 0), (0, cols - 1), (0, 0)))
    weights = weights + jnp.pad(south_fix[None], ((0, rows - 1), (0, 0), (0, 0)))
    weights = weights / cell_area[:, :, None]

    span = 7
    wide_cols = cols + 8
    grid = jnp.transpose(weights.reshape(rows, cols, span, span), (0, 2, 1, 3))
    grid = jnp.pad(grid, ((0, 0), (0, 0), (0, 0), (0, wide_cols + 1 - span)))
    grid = grid.reshape(rows, span, cols * (wide_cols + 1))[:, :, : cols * wide_cols]
    grid = grid.reshape(rows, span, cols, wide_cols)
    banded = jnp.stack(
        [jnp.pad(grid[i], ((i, rows - 1 - i), (0, 0), (0, 0))) for i in range(rows)], axis=0
    )
    banded = jnp.transpose(banded, (0, 2, 1, 3)).reshape(rows * cols, (rows + 6) * wide_cols)
    hi = lax.reduce_precision(banded, exponent_bits=8, mantissa_bits=7)
    rest = banded - hi
    mid = lax.reduce_precision(rest, exponent_bits=8, mantissa_bits=7)
    lo = rest - mid

    source = jnp.pad(padded, ((0, 0), (0, wide_cols - cols - 6), (0, 0))).reshape(-1, width)
    change = None
    for part in (hi, mid, lo):
        term = jnp.dot(part.astype(jnp.bfloat16), source, preferred_element_type=jnp.float32)
        change = term if change is None else change + term
    total = tracer.astype(jnp.float32) + change.reshape(rows, cols, width)
    return total.astype(jnp.bfloat16)


def solution(mesh):
    in_specs = (
        P("panel", "tile", None),
        P(None, "panel", "tile", None, None),
        P(None, "panel", "tile", None),
        P("panel", "tile"),
    )
    out_specs = P("panel", "tile", None)
    return jax.shard_map(local, mesh=mesh, in_specs=in_specs, out_specs=out_specs, check_vma=False)
```

```python
import functools
import math

import jax
import jax.numpy as jnp
import numpy as np
from jax import lax
from jax.experimental import pallas as pl
from jax.experimental.pallas import tpu as pltpu
from jax.sharding import PartitionSpec as P


INTERPRET = False


def from_prev(value, axis, wrap):
    size = lax.axis_size(axis)
    pairs = [(i, (i + 1) % size) for i in range(size if wrap else size - 1)]
    return lax.ppermute(value, axis, pairs)


def from_next(value, axis, wrap):
    size = lax.axis_size(axis)
    pairs = [((i + 1) % size, i) for i in range(size if wrap else size - 1)]
    return lax.ppermute(value, axis, pairs)


def stencil_table():
    stencil = np.zeros((6, 3, 3))
    stencil[0, 1, 1] = 7.0 / 6.0
    stencil[0, 1, 0] = -1.0 / 24.0
    stencil[0, 1, 2] = -1.0 / 24.0
    stencil[0, 0, 1] = -1.0 / 24.0
    stencil[0, 2, 1] = -1.0 / 24.0
    stencil[1, 1, 2] = 0.5
    stencil[1, 1, 0] = -0.5
    stencil[2, 2, 1] = 0.5
    stencil[2, 0, 1] = -0.5
    stencil[3, 1, 2] = 0.5
    stencil[3, 1, 0] = 0.5
    stencil[3, 1, 1] = -1.0
    stencil[4, 2, 2] = 0.25
    stencil[4, 2, 0] = -0.25
    stencil[4, 0, 2] = -0.25
    stencil[4, 0, 0] = 0.25
    stencil[5, 2, 1] = 0.5
    stencil[5, 0, 1] = 0.5
    stencil[5, 1, 1] = -1.0
    return stencil


def face_tables():
    stencil = stencil_table()
    tables = np.zeros((4, 12, 6, 7, 7))
    for face, (direction, shift_row, shift_col, sign) in enumerate(
        ((0, 0, -1, 1.0), (0, 0, 0, -1.0), (1, -1, 0, 1.0), (1, 0, 0, -1.0))
    ):
        for code in range(12):
            if direction == 0:
                row_off, col_off = code // 4 - 1, code % 4 - 1
            else:
                row_off, col_off = code % 4 - 1, code // 4 - 1
            for inner_row in range(-1, 2):
                for inner_col in range(-1, 2):
                    r = row_off + inner_row + shift_row + 3
                    c = col_off + inner_col + shift_col + 3
                    tables[face, code, :, r, c] += sign * stencil[:, inner_row + 1, inner_col + 1]
    tables = tables.reshape(4, 12, 6, 49)
    used = np.nonzero(np.abs(tables).sum(axis=(0, 1, 2)) > 0)[0]
    return tables[..., used], [(int(t) // 7 - 3, int(t) % 7 - 3) for t in used], tables


def summed_moments(pieces, moments):
    codes = jnp.arange(12, dtype=jnp.int32)
    onehot = (pieces[..., None] == codes).astype(jnp.float32)
    return jnp.einsum("...ko,...km->...om", onehot, moments, precision=lax.Precision.HIGHEST)


def split3(value):
    hi = lax.reduce_precision(value, exponent_bits=8, mantissa_bits=7)
    rest = value - hi
    mid = lax.reduce_precision(rest, exponent_bits=8, mantissa_bits=7)
    lo = rest - mid
    return jnp.concatenate([hi, mid, lo], axis=-1).astype(jnp.bfloat16)


def join3(value, count):
    parts = [value[..., k * count : (k + 1) * count].astype(jnp.float32) for k in range(3)]
    return (parts[0] + parts[1]) + parts[2]


def pack_weights(moments, pieces, width):
    lead = moments.shape[:-2]
    flat = moments.reshape(lead + (moments.shape[-2] * moments.shape[-1],))
    packed = jnp.concatenate([split3(flat), pieces.astype(jnp.bfloat16)], axis=-1)
    return jnp.pad(packed, [(0, 0)] * len(lead) + [(0, width - packed.shape[-1])])


def unpack_weights(packed, n_piece, n_moment):
    count = n_piece * n_moment
    lead = packed.shape[:-1]
    moments = join3(packed[..., : 3 * count], count).reshape(lead + (n_piece, n_moment))
    pieces = packed[..., 3 * count : 3 * count + n_piece].astype(jnp.int32)
    return moments, pieces


def face_weights(moments, pieces, tables):
    n_code = tables.shape[1]
    onehot = (pieces[..., None] == jnp.arange(n_code, dtype=jnp.int32)).astype(jnp.float32)
    spread = jnp.sum(onehot[..., :, None] * moments[..., None, :], axis=-3)
    lead = spread.shape[:-3]
    flat = spread.reshape(lead + (-1,))
    return jnp.dot(flat, tables.reshape(-1, tables.shape[-1]), precision=lax.Precision.HIGHEST)


def tap_sum(weights, padded, row0, col0, nrow, ncol, offsets, taps):
    total = None
    for tap in taps:
        dr, dc = offsets[tap]
        piece = lax.slice(
            padded, (3 + row0 + dr, 3 + col0 + dc, 0), (3 + row0 + dr + nrow, 3 + col0 + dc + ncol, padded.shape[2])
        )
        term = weights[:, :, tap][:, :, None] * piece.astype(jnp.float32)
        total = term if total is None else total + term
    return total


def tap_kernel(offsets, chunk, w_ref, p_ref, t_ref, o_ref, s_ref):
    s_ref[...] = p_ref[...].astype(jnp.float32)
    rows, cols, width = t_ref.shape

    def row(i, carry):
        for start in range(0, width, chunk):
            lanes = pl.ds(start, chunk)
            acc = t_ref[i, :, lanes].astype(jnp.float32)
            for tap, (dr, dc) in enumerate(offsets):
                w = w_ref[i, :, tap : tap + 1]
                acc = acc + w * s_ref[i + 3 + dr, pl.ds(3 + dc, cols), lanes]
            o_ref[i, :, lanes] = acc.astype(o_ref.dtype)
        return carry

    lax.fori_loop(0, rows, row, 0)


def apply_taps(weights, padded, tracer, offsets):
    return pl.pallas_call(
        functools.partial(tap_kernel, offsets, math.gcd(tracer.shape[2], 384)),
        out_shape=jax.ShapeDtypeStruct(tracer.shape, jnp.bfloat16),
        scratch_shapes=[pltpu.VMEM(padded.shape, jnp.float32)],
        interpret=INTERPRET,
    )(weights, padded, tracer)


def local(tracer, moments, pieces, cell_area):
    rows = tracer.shape[0]
    cols = tracer.shape[1]
    width = tracer.shape[2]
    n_piece = moments.shape[3]
    n_moment = moments.shape[4]
    np_tables, offsets, np_full = face_tables()
    tables = jnp.asarray(np_tables, jnp.float32)
    tables_full = jnp.asarray(np_full, jnp.float32)
    west_taps = [t for t in range(len(offsets)) if np.abs(np_tables[0, ..., t]).sum() > 0]
    south_taps = [t for t in range(len(offsets)) if np.abs(np_tables[2, ..., t]).sum() > 0]

    south_pack = pack_weights(moments[1][rows - 1], pieces[1][rows - 1], width)[None]
    from_south = from_prev(jnp.concatenate([tracer[rows - 3 :], south_pack], axis=0), "panel", False)
    from_north = from_next(tracer[:3], "panel", False)
    tall = jnp.concatenate([from_south[:3], tracer, from_north], axis=0)
    west_pack = jnp.pad(
        pack_weights(moments[0][:, cols - 1], pieces[0][:, cols - 1], width), ((3, 3), (0, 0))
    )[:, None]
    from_west = from_prev(jnp.concatenate([tall[:, cols - 3 :], west_pack], axis=1), "tile", True)
    from_east = from_next(tall[:, :3], "tile", True)
    padded = jnp.concatenate([from_west[:, :3], tall, from_east], axis=1)

    is_top = lax.axis_index("panel") == lax.axis_size("panel") - 1
    last_row = jnp.arange(rows) == rows - 1
    row_mask = jnp.where(jnp.logical_and(last_row, is_top), 0.0, 1.0).astype(jnp.float32)
    north_m = moments[1] * row_mask[:, None, None, None]
    zero_col = jnp.zeros_like(moments[0][:, :1])
    zero_row = jnp.zeros_like(moments[1][:1])
    face_m = jnp.stack(
        [
            jnp.concatenate([zero_col, moments[0][:, : cols - 1]], axis=1),
            moments[0],
            jnp.concatenate([zero_row, north_m[: rows - 1]], axis=0),
            north_m,
        ],
        axis=2,
    )
    face_p = jnp.stack(
        [
            jnp.concatenate([pieces[0][:, :1], pieces[0][:, : cols - 1]], axis=1),
            pieces[0],
            jnp.concatenate([pieces[1][:1], pieces[1][: rows - 1]], axis=0),
            pieces[1],
        ],
        axis=2,
    )
    weights = face_weights(face_m, face_p, tables_full) / cell_area[:, :, None]

    span = 7
    wide_cols = cols + 8
    grid = jnp.transpose(weights.reshape(rows, cols, span, span), (0, 2, 1, 3))
    grid = jnp.pad(grid, ((0, 0), (0, 0), (0, 0), (0, wide_cols + 1 - span)))
    grid = grid.reshape(rows, span, cols * (wide_cols + 1))[:, :, : cols * wide_cols]
    grid = grid.reshape(rows, span, cols, wide_cols)
    banded = jnp.stack(
        [jnp.pad(grid[i], ((i, rows - 1 - i), (0, 0), (0, 0))) for i in range(rows)], axis=0
    )
    banded = jnp.transpose(banded, (0, 2, 1, 3)).reshape(rows * cols, (rows + 6) * wide_cols)
    hi = lax.reduce_precision(banded, exponent_bits=8, mantissa_bits=7)
    rest = banded - hi
    mid = lax.reduce_precision(rest, exponent_bits=8, mantissa_bits=7)
    parts = jnp.stack([hi, mid, rest - mid]).astype(jnp.bfloat16)
    parts = lax.optimization_barrier(parts)

    west_m, west_p = unpack_weights(from_west[3 : 3 + rows, 3], n_piece, n_moment)
    south_m, south_p = unpack_weights(from_south[3], n_piece, n_moment)
    west_fix = face_weights(west_m[:, None], west_p[:, None], tables[:1]) / cell_area[:, :1]
    south_fix = face_weights(south_m[:, None], south_p[:, None], tables[2:3]) / cell_area[0][:, None]

    source = jnp.pad(padded, ((0, 0), (0, wide_cols - cols - 6), (0, 0))).reshape(-1, width)
    change = None
    for k in range(3):
        term = jnp.dot(parts[k], source, preferred_element_type=jnp.float32)
        change = term if change is None else change + term
    total = tracer.astype(jnp.float32) + change.reshape(rows, cols, width)
    west_add = tap_sum(west_fix[:, None], padded, 0, 0, rows, 1, offsets, west_taps)
    south_add = tap_sum(south_fix[None], padded, 0, 0, 1, cols, offsets, south_taps)
    total = total + jnp.pad(west_add, ((0, 0), (0, cols - 1), (0, 0)))
    total = total + jnp.pad(south_add, ((0, rows - 1), (0, 0), (0, 0)))
    return total.astype(jnp.bfloat16)


def solution(mesh):
    in_specs = (
        P("panel", "tile", None),
        P(None, "panel", "tile", None, None),
        P(None, "panel", "tile", None),
        P("panel", "tile"),
    )
    out_specs = P("panel", "tile", None)
    return jax.shard_map(local, mesh=mesh, in_specs=in_specs, out_specs=out_specs, check_vma=False)
```

```python
import functools
import math

import jax
import jax.numpy as jnp
import numpy as np
from jax import lax
from jax.experimental import pallas as pl
from jax.experimental.pallas import tpu as pltpu
from jax.sharding import PartitionSpec as P


INTERPRET = False


def from_prev(value, axis, wrap):
    size = lax.axis_size(axis)
    pairs = [(i, (i + 1) % size) for i in range(size if wrap else size - 1)]
    return lax.ppermute(value, axis, pairs)


def from_next(value, axis, wrap):
    size = lax.axis_size(axis)
    pairs = [((i + 1) % size, i) for i in range(size if wrap else size - 1)]
    return lax.ppermute(value, axis, pairs)


def stencil_table():
    stencil = np.zeros((6, 3, 3))
    stencil[0, 1, 1] = 7.0 / 6.0
    stencil[0, 1, 0] = -1.0 / 24.0
    stencil[0, 1, 2] = -1.0 / 24.0
    stencil[0, 0, 1] = -1.0 / 24.0
    stencil[0, 2, 1] = -1.0 / 24.0
    stencil[1, 1, 2] = 0.5
    stencil[1, 1, 0] = -0.5
    stencil[2, 2, 1] = 0.5
    stencil[2, 0, 1] = -0.5
    stencil[3, 1, 2] = 0.5
    stencil[3, 1, 0] = 0.5
    stencil[3, 1, 1] = -1.0
    stencil[4, 2, 2] = 0.25
    stencil[4, 2, 0] = -0.25
    stencil[4, 0, 2] = -0.25
    stencil[4, 0, 0] = 0.25
    stencil[5, 2, 1] = 0.5
    stencil[5, 0, 1] = 0.5
    stencil[5, 1, 1] = -1.0
    return stencil


def face_tables():
    stencil = stencil_table()
    tables = np.zeros((4, 12, 6, 7, 7))
    for face, (direction, shift_row, shift_col, sign) in enumerate(
        ((0, 0, -1, 1.0), (0, 0, 0, -1.0), (1, -1, 0, 1.0), (1, 0, 0, -1.0))
    ):
        for code in range(12):
            if direction == 0:
                row_off, col_off = code // 4 - 1, code % 4 - 1
            else:
                row_off, col_off = code % 4 - 1, code // 4 - 1
            for inner_row in range(-1, 2):
                for inner_col in range(-1, 2):
                    r = row_off + inner_row + shift_row + 3
                    c = col_off + inner_col + shift_col + 3
                    tables[face, code, :, r, c] += sign * stencil[:, inner_row + 1, inner_col + 1]
    tables = tables.reshape(4, 12, 6, 49)
    used = np.nonzero(np.abs(tables).sum(axis=(0, 1, 2)) > 0)[0]
    return tables[..., used], [(int(t) // 7 - 3, int(t) % 7 - 3) for t in used]


def summed_moments(pieces, moments):
    codes = jnp.arange(12, dtype=jnp.int32)
    onehot = (pieces[..., None] == codes).astype(jnp.float32)
    return jnp.einsum("...ko,...km->...om", onehot, moments, precision=lax.Precision.HIGHEST)


def split3(value):
    hi = lax.reduce_precision(value, exponent_bits=8, mantissa_bits=7)
    rest = value - hi
    mid = lax.reduce_precision(rest, exponent_bits=8, mantissa_bits=7)
    lo = rest - mid
    return jnp.concatenate([hi, mid, lo], axis=-1).astype(jnp.bfloat16)


def join3(value, count):
    parts = [value[..., k * count : (k + 1) * count].astype(jnp.float32) for k in range(3)]
    return (parts[0] + parts[1]) + parts[2]


def pack_weights(moments, pieces, width):
    lead = moments.shape[:-2]
    flat = moments.reshape(lead + (moments.shape[-2] * moments.shape[-1],))
    packed = jnp.concatenate([split3(flat), pieces.astype(jnp.bfloat16)], axis=-1)
    return jnp.pad(packed, [(0, 0)] * len(lead) + [(0, width - packed.shape[-1])])


def unpack_weights(packed, n_piece, n_moment):
    count = n_piece * n_moment
    lead = packed.shape[:-1]
    moments = join3(packed[..., : 3 * count], count).reshape(lead + (n_piece, n_moment))
    pieces = packed[..., 3 * count : 3 * count + n_piece].astype(jnp.int32)
    return moments, pieces


def face_weights(moments, pieces, tables):
    n_code = tables.shape[1]
    onehot = (pieces[..., None] == jnp.arange(n_code, dtype=jnp.int32)).astype(jnp.float32)
    spread = jnp.sum(onehot[..., :, None] * moments[..., None, :], axis=-3)
    lead = spread.shape[:-3]
    flat = spread.reshape(lead + (-1,))
    return jnp.dot(flat, tables.reshape(-1, tables.shape[-1]), precision=lax.Precision.HIGHEST)


def tap_sum(weights, padded, row0, col0, nrow, ncol, offsets, taps):
    total = None
    for tap in taps:
        dr, dc = offsets[tap]
        piece = lax.slice(
            padded, (3 + row0 + dr, 3 + col0 + dc, 0), (3 + row0 + dr + nrow, 3 + col0 + dc + ncol, padded.shape[2])
        )
        term = weights[:, :, tap][:, :, None] * piece.astype(jnp.float32)
        total = term if total is None else total + term
    return total


def tap_kernel(offsets, chunk, w_ref, p_ref, t_ref, o_ref, s_ref):
    s_ref[...] = p_ref[...].astype(jnp.float32)
    rows, cols, width = t_ref.shape

    def row(i, carry):
        for start in range(0, width, chunk):
            lanes = pl.ds(start, chunk)
            acc = t_ref[i, :, lanes].astype(jnp.float32)
            for tap, (dr, dc) in enumerate(offsets):
                w = w_ref[i, :, tap : tap + 1]
                acc = acc + w * s_ref[i + 3 + dr, pl.ds(3 + dc, cols), lanes]
            o_ref[i, :, lanes] = acc.astype(o_ref.dtype)
        return carry

    lax.fori_loop(0, rows, row, 0)


def apply_taps(weights, padded, tracer, offsets):
    return pl.pallas_call(
        functools.partial(tap_kernel, offsets, tracer.shape[2]),
        out_shape=jax.ShapeDtypeStruct(tracer.shape, jnp.bfloat16),
        scratch_shapes=[pltpu.VMEM(padded.shape, jnp.float32)],
        interpret=INTERPRET,
    )(weights, padded, tracer)


def local(tracer, moments, pieces, cell_area):
    rows = tracer.shape[0]
    cols = tracer.shape[1]
    width = tracer.shape[2]
    n_piece = moments.shape[3]
    n_moment = moments.shape[4]
    np_tables, offsets = face_tables()
    tables = jnp.asarray(np_tables, jnp.float32)
    west_taps = [t for t in range(len(offsets)) if np.abs(np_tables[0, ..., t]).sum() > 0]
    south_taps = [t for t in range(len(offsets)) if np.abs(np_tables[2, ..., t]).sum() > 0]

    south_pack = pack_weights(moments[1][rows - 1], pieces[1][rows - 1], width)[None]
    from_south = from_prev(jnp.concatenate([tracer[rows - 3 :], south_pack], axis=0), "panel", False)
    from_north = from_next(tracer[:3], "panel", False)
    tall = jnp.concatenate([from_south[:3], tracer, from_north], axis=0)
    west_pack = jnp.pad(
        pack_weights(moments[0][:, cols - 1], pieces[0][:, cols - 1], width), ((3, 3), (0, 0))
    )[:, None]
    from_west = from_prev(jnp.concatenate([tall[:, cols - 3 :], west_pack], axis=1), "tile", True)
    from_east = from_next(tall[:, :3], "tile", True)
    padded = jnp.concatenate([from_west[:, :3], tall, from_east], axis=1)

    is_top = lax.axis_index("panel") == lax.axis_size("panel") - 1
    last_row = jnp.arange(rows) == rows - 1
    row_mask = jnp.where(jnp.logical_and(last_row, is_top), 0.0, 1.0).astype(jnp.float32)
    north_m = moments[1] * row_mask[:, None, None, None]
    zero_col = jnp.zeros_like(moments[0][:, :1])
    zero_row = jnp.zeros_like(moments[1][:1])
    face_m = jnp.stack(
        [
            jnp.concatenate([zero_col, moments[0][:, : cols - 1]], axis=1),
            moments[0],
            jnp.concatenate([zero_row, north_m[: rows - 1]], axis=0),
            north_m,
        ],
        axis=2,
    )
    face_p = jnp.stack(
        [
            jnp.concatenate([pieces[0][:, :1], pieces[0][:, : cols - 1]], axis=1),
            pieces[0],
            jnp.concatenate([pieces[1][:1], pieces[1][: rows - 1]], axis=0),
            pieces[1],
        ],
        axis=2,
    )
    weights = face_weights(face_m, face_p, tables)
    weights = lax.optimization_barrier(weights)

    west_m, west_p = unpack_weights(from_west[3 : 3 + rows, 3], n_piece, n_moment)
    south_m, south_p = unpack_weights(from_south[3], n_piece, n_moment)
    west_fix = face_weights(west_m[:, None], west_p[:, None], tables[:1])
    south_fix = face_weights(south_m[:, None], south_p[:, None], tables[2:3])
    weights = weights + jnp.pad(west_fix[:, None], ((0, 0), (0, cols - 1), (0, 0)))
    weights = weights + jnp.pad(south_fix[None], ((0, rows - 1), (0, 0), (0, 0)))
    weights = weights / cell_area[:, :, None]
    return apply_taps(weights, padded, tracer, offsets)


def solution(mesh):
    in_specs = (
        P("panel", "tile", None),
        P(None, "panel", "tile", None, None),
        P(None, "panel", "tile", None),
        P("panel", "tile"),
    )
    out_specs = P("panel", "tile", None)
    return jax.shard_map(local, mesh=mesh, in_specs=in_specs, out_specs=out_specs, check_vma=False)
```

```python
import functools
import math

import jax
import jax.numpy as jnp
import numpy as np
from jax import lax
from jax.experimental import pallas as pl
from jax.experimental.pallas import tpu as pltpu
from jax.sharding import PartitionSpec as P


INTERPRET = False


def from_prev(value, axis, wrap):
    size = lax.axis_size(axis)
    pairs = [(i, (i + 1) % size) for i in range(size if wrap else size - 1)]
    return lax.ppermute(value, axis, pairs)


def from_next(value, axis, wrap):
    size = lax.axis_size(axis)
    pairs = [((i + 1) % size, i) for i in range(size if wrap else size - 1)]
    return lax.ppermute(value, axis, pairs)


def stencil_table():
    stencil = np.zeros((6, 3, 3))
    stencil[0, 1, 1] = 7.0 / 6.0
    stencil[0, 1, 0] = -1.0 / 24.0
    stencil[0, 1, 2] = -1.0 / 24.0
    stencil[0, 0, 1] = -1.0 / 24.0
    stencil[0, 2, 1] = -1.0 / 24.0
    stencil[1, 1, 2] = 0.5
    stencil[1, 1, 0] = -0.5
    stencil[2, 2, 1] = 0.5
    stencil[2, 0, 1] = -0.5
    stencil[3, 1, 2] = 0.5
    stencil[3, 1, 0] = 0.5
    stencil[3, 1, 1] = -1.0
    stencil[4, 2, 2] = 0.25
    stencil[4, 2, 0] = -0.25
    stencil[4, 0, 2] = -0.25
    stencil[4, 0, 0] = 0.25
    stencil[5, 2, 1] = 0.5
    stencil[5, 0, 1] = 0.5
    stencil[5, 1, 1] = -1.0
    return stencil


def face_tables():
    stencil = stencil_table()
    tables = np.zeros((4, 12, 6, 7, 7))
    for face, (direction, shift_row, shift_col, sign) in enumerate(
        ((0, 0, -1, 1.0), (0, 0, 0, -1.0), (1, -1, 0, 1.0), (1, 0, 0, -1.0))
    ):
        for code in range(12):
            if direction == 0:
                row_off, col_off = code // 4 - 1, code % 4 - 1
            else:
                row_off, col_off = code % 4 - 1, code // 4 - 1
            for inner_row in range(-1, 2):
                for inner_col in range(-1, 2):
                    r = row_off + inner_row + shift_row + 3
                    c = col_off + inner_col + shift_col + 3
                    tables[face, code, :, r, c] += sign * stencil[:, inner_row + 1, inner_col + 1]
    tables = tables.reshape(4, 12, 6, 49)
    used = np.nonzero(np.abs(tables).sum(axis=(0, 1, 2)) > 0)[0]
    return tables[..., used], [(int(t) // 7 - 3, int(t) % 7 - 3) for t in used]


def summed_moments(pieces, moments):
    codes = jnp.arange(12, dtype=jnp.int32)
    onehot = (pieces[..., None] == codes).astype(jnp.float32)
    return jnp.einsum("...ko,...km->...om", onehot, moments, precision=lax.Precision.HIGHEST)


def split3(value):
    hi = lax.reduce_precision(value, exponent_bits=8, mantissa_bits=7)
    rest = value - hi
    mid = lax.reduce_precision(rest, exponent_bits=8, mantissa_bits=7)
    lo = rest - mid
    return jnp.concatenate([hi, mid, lo], axis=-1).astype(jnp.bfloat16)


def join3(value, count):
    parts = [value[..., k * count : (k + 1) * count].astype(jnp.float32) for k in range(3)]
    return (parts[0] + parts[1]) + parts[2]


def pack_weights(moments, pieces, width):
    lead = moments.shape[:-2]
    flat = moments.reshape(lead + (moments.shape[-2] * moments.shape[-1],))
    packed = jnp.concatenate([split3(flat), pieces.astype(jnp.bfloat16)], axis=-1)
    return jnp.pad(packed, [(0, 0)] * len(lead) + [(0, width - packed.shape[-1])])


def unpack_weights(packed, n_piece, n_moment):
    count = n_piece * n_moment
    lead = packed.shape[:-1]
    moments = join3(packed[..., : 3 * count], count).reshape(lead + (n_piece, n_moment))
    pieces = packed[..., 3 * count : 3 * count + n_piece].astype(jnp.int32)
    return moments, pieces


def face_weights(moments, pieces, tables):
    n_code = tables.shape[1]
    onehot = (pieces[..., None] == jnp.arange(n_code, dtype=jnp.int32)).astype(jnp.float32)
    spread = jnp.sum(onehot[..., :, None] * moments[..., None, :], axis=-3)
    lead = spread.shape[:-3]
    flat = spread.reshape(lead + (-1,))
    return jnp.dot(flat, tables.reshape(-1, tables.shape[-1]), precision=lax.Precision.HIGHEST)


def tap_sum(weights, padded, row0, col0, nrow, ncol, offsets, taps):
    total = None
    for tap in taps:
        dr, dc = offsets[tap]
        piece = lax.slice(
            padded, (3 + row0 + dr, 3 + col0 + dc, 0), (3 + row0 + dr + nrow, 3 + col0 + dc + ncol, padded.shape[2])
        )
        term = weights[:, :, tap][:, :, None] * piece.astype(jnp.float32)
        total = term if total is None else total + term
    return total


def face_weights_cells(moments, pieces, tables):
    n_row, n_col = moments.shape[:2]
    n_code = tables.shape[1]
    m_t = jnp.transpose(moments, (2, 3, 4, 0, 1)).reshape(moments.shape[2:] + (n_row * n_col,))
    p_t = jnp.transpose(pieces, (2, 3, 0, 1)).reshape(pieces.shape[2:] + (n_row * n_col,))
    onehot = (p_t[:, :, None, :] == jnp.arange(n_code, dtype=jnp.int32)[None, None, :, None]).astype(jnp.float32)
    spread = jnp.sum(onehot[:, :, :, None, :] * m_t[:, :, None, :, :], axis=1)
    flat = spread.reshape(-1, n_row * n_col).T
    scaled = jnp.round(tables * 24.0).reshape(-1, tables.shape[-1])
    weights = jnp.dot(flat, scaled, precision=lax.Precision.HIGH) / 24.0
    return weights.reshape(n_row, n_col, tables.shape[-1])


def tap_kernel(offsets, chunk, w_ref, p_ref, t_ref, o_ref, s_ref):
    s_ref[...] = p_ref[...].astype(jnp.float32)
    rows, cols, width = t_ref.shape

    def row(i, carry):
        for start in range(0, width, chunk):
            lanes = pl.ds(start, chunk)
            acc = t_ref[i, :, lanes].astype(jnp.float32)
            for tap, (dr, dc) in enumerate(offsets):
                w = w_ref[i, :, tap : tap + 1]
                acc = acc + w * s_ref[i + 3 + dr, pl.ds(3 + dc, cols), lanes]
            o_ref[i, :, lanes] = acc.astype(o_ref.dtype)
        return carry

    lax.fori_loop(0, rows, row, 0)


def apply_taps(weights, padded, tracer, offsets):
    return pl.pallas_call(
        functools.partial(tap_kernel, offsets, tracer.shape[2]),
        out_shape=jax.ShapeDtypeStruct(tracer.shape, jnp.bfloat16),
        scratch_shapes=[pltpu.VMEM(padded.shape, jnp.float32)],
        interpret=INTERPRET,
    )(weights, padded, tracer)


def local(tracer, moments, pieces, cell_area):
    rows = tracer.shape[0]
    cols = tracer.shape[1]
    width = tracer.shape[2]
    n_piece = moments.shape[3]
    n_moment = moments.shape[4]
    np_tables, offsets = face_tables()
    tables = jnp.asarray(np_tables, jnp.float32)
    west_taps = [t for t in range(len(offsets)) if np.abs(np_tables[0, ..., t]).sum() > 0]
    south_taps = [t for t in range(len(offsets)) if np.abs(np_tables[2, ..., t]).sum() > 0]

    south_pack = pack_weights(moments[1][rows - 1], pieces[1][rows - 1], width)[None]
    from_south = from_prev(jnp.concatenate([tracer[rows - 3 :], south_pack], axis=0), "panel", False)
    from_north = from_next(tracer[:3], "panel", False)
    tall = jnp.concatenate([from_south[:3], tracer, from_north], axis=0)
    west_pack = jnp.pad(
        pack_weights(moments[0][:, cols - 1], pieces[0][:, cols - 1], width), ((3, 3), (0, 0))
    )[:, None]
    from_west = from_prev(jnp.concatenate([tall[:, cols - 3 :], west_pack], axis=1), "tile", True)
    from_east = from_next(tall[:, :3], "tile", True)
    padded = jnp.concatenate([from_west[:, :3], tall, from_east], axis=1)

    is_top = lax.axis_index("panel") == lax.axis_size("panel") - 1
    last_row = jnp.arange(rows) == rows - 1
    row_mask = jnp.where(jnp.logical_and(last_row, is_top), 0.0, 1.0).astype(jnp.float32)
    north_m = moments[1] * row_mask[:, None, None, None]
    zero_col = jnp.zeros_like(moments[0][:, :1])
    zero_row = jnp.zeros_like(moments[1][:1])
    face_m = jnp.stack(
        [
            jnp.concatenate([zero_col, moments[0][:, : cols - 1]], axis=1),
            moments[0],
            jnp.concatenate([zero_row, north_m[: rows - 1]], axis=0),
            north_m,
        ],
        axis=2,
    )
    face_p = jnp.stack(
        [
            jnp.concatenate([pieces[0][:, :1], pieces[0][:, : cols - 1]], axis=1),
            pieces[0],
            jnp.concatenate([pieces[1][:1], pieces[1][: rows - 1]], axis=0),
            pieces[1],
        ],
        axis=2,
    )
    weights = face_weights_cells(face_m, face_p, tables)
    weights = lax.optimization_barrier(weights)

    west_m, west_p = unpack_weights(from_west[3 : 3 + rows, 3], n_piece, n_moment)
    south_m, south_p = unpack_weights(from_south[3], n_piece, n_moment)
    west_fix = face_weights(west_m[:, None], west_p[:, None], tables[:1])
    south_fix = face_weights(south_m[:, None], south_p[:, None], tables[2:3])
    weights = weights + jnp.pad(west_fix[:, None], ((0, 0), (0, cols - 1), (0, 0)))
    weights = weights + jnp.pad(south_fix[None], ((0, rows - 1), (0, 0), (0, 0)))
    weights = weights / cell_area[:, :, None]
    return apply_taps(weights, padded, tracer, offsets)


def solution(mesh):
    in_specs = (
        P("panel", "tile", None),
        P(None, "panel", "tile", None, None),
        P(None, "panel", "tile", None),
        P("panel", "tile"),
    )
    out_specs = P("panel", "tile", None)
    return jax.shard_map(local, mesh=mesh, in_specs=in_specs, out_specs=out_specs, check_vma=False)
```

```python
import functools
import math

import jax
import jax.numpy as jnp
import numpy as np
from jax import lax
from jax.experimental import pallas as pl
from jax.experimental.pallas import tpu as pltpu
from jax.sharding import PartitionSpec as P


INTERPRET = False


def from_prev(value, axis, wrap):
    size = lax.axis_size(axis)
    pairs = [(i, (i + 1) % size) for i in range(size if wrap else size - 1)]
    return lax.ppermute(value, axis, pairs)


def from_next(value, axis, wrap):
    size = lax.axis_size(axis)
    pairs = [((i + 1) % size, i) for i in range(size if wrap else size - 1)]
    return lax.ppermute(value, axis, pairs)


def stencil_table():
    stencil = np.zeros((6, 3, 3))
    stencil[0, 1, 1] = 7.0 / 6.0
    stencil[0, 1, 0] = -1.0 / 24.0
    stencil[0, 1, 2] = -1.0 / 24.0
    stencil[0, 0, 1] = -1.0 / 24.0
    stencil[0, 2, 1] = -1.0 / 24.0
    stencil[1, 1, 2] = 0.5
    stencil[1, 1, 0] = -0.5
    stencil[2, 2, 1] = 0.5
    stencil[2, 0, 1] = -0.5
    stencil[3, 1, 2] = 0.5
    stencil[3, 1, 0] = 0.5
    stencil[3, 1, 1] = -1.0
    stencil[4, 2, 2] = 0.25
    stencil[4, 2, 0] = -0.25
    stencil[4, 0, 2] = -0.25
    stencil[4, 0, 0] = 0.25
    stencil[5, 2, 1] = 0.5
    stencil[5, 0, 1] = 0.5
    stencil[5, 1, 1] = -1.0
    return stencil


def face_tables():
    stencil = stencil_table()
    tables = np.zeros((4, 12, 6, 7, 7))
    for face, (direction, shift_row, shift_col, sign) in enumerate(
        ((0, 0, -1, 1.0), (0, 0, 0, -1.0), (1, -1, 0, 1.0), (1, 0, 0, -1.0))
    ):
        for code in range(12):
            if direction == 0:
                row_off, col_off = code // 4 - 1, code % 4 - 1
            else:
                row_off, col_off = code % 4 - 1, code // 4 - 1
            for inner_row in range(-1, 2):
                for inner_col in range(-1, 2):
                    r = row_off + inner_row + shift_row + 3
                    c = col_off + inner_col + shift_col + 3
                    tables[face, code, :, r, c] += sign * stencil[:, inner_row + 1, inner_col + 1]
    tables = tables.reshape(4, 12, 6, 49)
    used = np.nonzero(np.abs(tables).sum(axis=(0, 1, 2)) > 0)[0]
    return tables[..., used], [(int(t) // 7 - 3, int(t) % 7 - 3) for t in used]


def summed_moments(pieces, moments):
    codes = jnp.arange(12, dtype=jnp.int32)
    onehot = (pieces[..., None] == codes).astype(jnp.float32)
    return jnp.einsum("...ko,...km->...om", onehot, moments, precision=lax.Precision.HIGHEST)


def split3(value):
    hi = lax.reduce_precision(value, exponent_bits=8, mantissa_bits=7)
    rest = value - hi
    mid = lax.reduce_precision(rest, exponent_bits=8, mantissa_bits=7)
    lo = rest - mid
    return jnp.concatenate([hi, mid, lo], axis=-1).astype(jnp.bfloat16)


def join3(value, count):
    parts = [value[..., k * count : (k + 1) * count].astype(jnp.float32) for k in range(3)]
    return (parts[0] + parts[1]) + parts[2]


def pack_weights(moments, pieces, width):
    lead = moments.shape[:-2]
    flat = moments.reshape(lead + (moments.shape[-2] * moments.shape[-1],))
    packed = jnp.concatenate([split3(flat), pieces.astype(jnp.bfloat16)], axis=-1)
    return jnp.pad(packed, [(0, 0)] * len(lead) + [(0, width - packed.shape[-1])])


def unpack_weights(packed, n_piece, n_moment):
    count = n_piece * n_moment
    lead = packed.shape[:-1]
    moments = join3(packed[..., : 3 * count], count).reshape(lead + (n_piece, n_moment))
    pieces = packed[..., 3 * count : 3 * count + n_piece].astype(jnp.int32)
    return moments, pieces


def face_weights(moments, pieces, tables):
    n_code = tables.shape[1]
    onehot = (pieces[..., None] == jnp.arange(n_code, dtype=jnp.int32)).astype(jnp.float32)
    spread = jnp.sum(onehot[..., :, None] * moments[..., None, :], axis=-3)
    lead = spread.shape[:-3]
    flat = spread.reshape(lead + (-1,))
    return jnp.dot(flat, tables.reshape(-1, tables.shape[-1]), precision=lax.Precision.HIGHEST)


def tap_sum(weights, padded, row0, col0, nrow, ncol, offsets, taps):
    total = None
    for tap in taps:
        dr, dc = offsets[tap]
        piece = lax.slice(
            padded, (3 + row0 + dr, 3 + col0 + dc, 0), (3 + row0 + dr + nrow, 3 + col0 + dc + ncol, padded.shape[2])
        )
        term = weights[:, :, tap][:, :, None] * piece.astype(jnp.float32)
        total = term if total is None else total + term
    return total


def face_weights_cells(moments, pieces, tables):
    n_row, n_col = moments.shape[:2]
    n_code = tables.shape[1]
    m_t = jnp.transpose(moments, (2, 3, 4, 0, 1)).reshape(moments.shape[2:] + (n_row * n_col,))
    p_t = jnp.transpose(pieces, (2, 3, 0, 1)).reshape(pieces.shape[2:] + (n_row * n_col,))
    onehot = (p_t[:, :, None, :] == jnp.arange(n_code, dtype=jnp.int32)[None, None, :, None]).astype(jnp.float32)
    spread = jnp.sum(onehot[:, :, :, None, :] * m_t[:, :, None, :, :], axis=1)
    flat = spread.reshape(-1, n_row * n_col).T
    scaled = jnp.round(tables * 24.0).reshape(-1, tables.shape[-1])
    weights = jnp.dot(flat, scaled, precision=lax.Precision.HIGH) / 24.0
    return weights.reshape(n_row, n_col, tables.shape[-1])


def tap_kernel(offsets, chunk, w_ref, south_ref, t_ref, north_ref, west_ref, east_ref, o_ref, s_ref):
    rows, cols, width = t_ref.shape
    halo = north_ref.shape[0]
    f32 = jnp.float32
    s_ref[0:halo, halo : halo + cols] = south_ref[0:halo].astype(f32)
    s_ref[halo : halo + rows, halo : halo + cols] = t_ref[...].astype(f32)
    s_ref[halo + rows :, halo : halo + cols] = north_ref[...].astype(f32)
    s_ref[:, 0:halo] = west_ref[:, 0:halo].astype(f32)
    s_ref[:, halo + cols :] = east_ref[...].astype(f32)

    def row(i, carry):
        for start in range(0, width, chunk):
            lanes = pl.ds(start, chunk)
            acc = s_ref[i + halo, pl.ds(halo, cols), lanes]
            for tap, (dr, dc) in enumerate(offsets):
                w = w_ref[i, :, tap : tap + 1]
                acc = acc + w * s_ref[i + halo + dr, pl.ds(halo + dc, cols), lanes]
            o_ref[i, :, lanes] = acc.astype(o_ref.dtype)
        return carry

    lax.fori_loop(0, rows, row, 0)


def apply_taps(weights, from_south, tracer, from_north, from_west, from_east, offsets):
    rows, cols, width = tracer.shape
    halo = from_north.shape[0]
    return pl.pallas_call(
        functools.partial(tap_kernel, offsets, width),
        out_shape=jax.ShapeDtypeStruct(tracer.shape, jnp.bfloat16),
        scratch_shapes=[pltpu.VMEM((rows + 2 * halo, cols + 2 * halo, width), jnp.float32)],
        interpret=INTERPRET,
    )(weights, from_south, tracer, from_north, from_west, from_east)


def local(tracer, moments, pieces, cell_area):
    rows = tracer.shape[0]
    cols = tracer.shape[1]
    width = tracer.shape[2]
    n_piece = moments.shape[3]
    n_moment = moments.shape[4]
    np_tables, offsets = face_tables()
    tables = jnp.asarray(np_tables, jnp.float32)
    west_taps = [t for t in range(len(offsets)) if np.abs(np_tables[0, ..., t]).sum() > 0]
    south_taps = [t for t in range(len(offsets)) if np.abs(np_tables[2, ..., t]).sum() > 0]

    south_pack = pack_weights(moments[1][rows - 1], pieces[1][rows - 1], width)[None]
    from_south = from_prev(jnp.concatenate([tracer[rows - 3 :], south_pack], axis=0), "panel", False)
    from_north = from_next(tracer[:3], "panel", False)
    tall = jnp.concatenate([from_south[:3], tracer, from_north], axis=0)
    west_pack = jnp.pad(
        pack_weights(moments[0][:, cols - 1], pieces[0][:, cols - 1], width), ((3, 3), (0, 0))
    )[:, None]
    from_west = from_prev(jnp.concatenate([tall[:, cols - 3 :], west_pack], axis=1), "tile", True)
    from_east = from_next(tall[:, :3], "tile", True)

    is_top = lax.axis_index("panel") == lax.axis_size("panel") - 1
    last_row = jnp.arange(rows) == rows - 1
    row_mask = jnp.where(jnp.logical_and(last_row, is_top), 0.0, 1.0).astype(jnp.float32)
    north_m = moments[1] * row_mask[:, None, None, None]
    zero_col = jnp.zeros_like(moments[0][:, :1])
    zero_row = jnp.zeros_like(moments[1][:1])
    face_m = jnp.stack(
        [
            jnp.concatenate([zero_col, moments[0][:, : cols - 1]], axis=1),
            moments[0],
            jnp.concatenate([zero_row, north_m[: rows - 1]], axis=0),
            north_m,
        ],
        axis=2,
    )
    face_p = jnp.stack(
        [
            jnp.concatenate([pieces[0][:, :1], pieces[0][:, : cols - 1]], axis=1),
            pieces[0],
            jnp.concatenate([pieces[1][:1], pieces[1][: rows - 1]], axis=0),
            pieces[1],
        ],
        axis=2,
    )
    weights = face_weights_cells(face_m, face_p, tables)
    weights = lax.optimization_barrier(weights)

    west_m, west_p = unpack_weights(from_west[3 : 3 + rows, 3], n_piece, n_moment)
    south_m, south_p = unpack_weights(from_south[3], n_piece, n_moment)
    west_fix = face_weights(west_m[:, None], west_p[:, None], tables[:1])
    south_fix = face_weights(south_m[:, None], south_p[:, None], tables[2:3])
    weights = weights + jnp.pad(west_fix[:, None], ((0, 0), (0, cols - 1), (0, 0)))
    weights = weights + jnp.pad(south_fix[None], ((0, rows - 1), (0, 0), (0, 0)))
    weights = weights / cell_area[:, :, None]
    return apply_taps(weights, from_south, tracer, from_north, from_west, from_east, offsets)


def solution(mesh):
    in_specs = (
        P("panel", "tile", None),
        P(None, "panel", "tile", None, None),
        P(None, "panel", "tile", None),
        P("panel", "tile"),
    )
    out_specs = P("panel", "tile", None)
    return jax.shard_map(local, mesh=mesh, in_specs=in_specs, out_specs=out_specs, check_vma=False)
```

```python
import functools
import math

import jax
import jax.numpy as jnp
import numpy as np
from jax import lax
from jax.experimental import pallas as pl
from jax.experimental.pallas import tpu as pltpu
from jax.sharding import PartitionSpec as P


INTERPRET = False


def from_prev(value, axis, wrap):
    size = lax.axis_size(axis)
    pairs = [(i, (i + 1) % size) for i in range(size if wrap else size - 1)]
    return lax.ppermute(value, axis, pairs)


def from_next(value, axis, wrap):
    size = lax.axis_size(axis)
    pairs = [((i + 1) % size, i) for i in range(size if wrap else size - 1)]
    return lax.ppermute(value, axis, pairs)


def stencil_table():
    stencil = np.zeros((6, 3, 3))
    stencil[0, 1, 1] = 7.0 / 6.0
    stencil[0, 1, 0] = -1.0 / 24.0
    stencil[0, 1, 2] = -1.0 / 24.0
    stencil[0, 0, 1] = -1.0 / 24.0
    stencil[0, 2, 1] = -1.0 / 24.0
    stencil[1, 1, 2] = 0.5
    stencil[1, 1, 0] = -0.5
    stencil[2, 2, 1] = 0.5
    stencil[2, 0, 1] = -0.5
    stencil[3, 1, 2] = 0.5
    stencil[3, 1, 0] = 0.5
    stencil[3, 1, 1] = -1.0
    stencil[4, 2, 2] = 0.25
    stencil[4, 2, 0] = -0.25
    stencil[4, 0, 2] = -0.25
    stencil[4, 0, 0] = 0.25
    stencil[5, 2, 1] = 0.5
    stencil[5, 0, 1] = 0.5
    stencil[5, 1, 1] = -1.0
    return stencil


def face_tables():
    stencil = stencil_table()
    tables = np.zeros((4, 12, 6, 7, 7))
    for face, (direction, shift_row, shift_col, sign) in enumerate(
        ((0, 0, -1, 1.0), (0, 0, 0, -1.0), (1, -1, 0, 1.0), (1, 0, 0, -1.0))
    ):
        for code in range(12):
            if direction == 0:
                row_off, col_off = code // 4 - 1, code % 4 - 1
            else:
                row_off, col_off = code % 4 - 1, code // 4 - 1
            for inner_row in range(-1, 2):
                for inner_col in range(-1, 2):
                    r = row_off + inner_row + shift_row + 3
                    c = col_off + inner_col + shift_col + 3
                    tables[face, code, :, r, c] += sign * stencil[:, inner_row + 1, inner_col + 1]
    tables = tables.reshape(4, 12, 6, 49)
    used = np.nonzero(np.abs(tables).sum(axis=(0, 1, 2)) > 0)[0]
    return tables[..., used], [(int(t) // 7 - 3, int(t) % 7 - 3) for t in used]


def summed_moments(pieces, moments):
    codes = jnp.arange(12, dtype=jnp.int32)
    onehot = (pieces[..., None] == codes).astype(jnp.float32)
    return jnp.einsum("...ko,...km->...om", onehot, moments, precision=lax.Precision.HIGHEST)


def split3(value):
    hi = lax.reduce_precision(value, exponent_bits=8, mantissa_bits=7)
    rest = value - hi
    mid = lax.reduce_precision(rest, exponent_bits=8, mantissa_bits=7)
    lo = rest - mid
    return jnp.concatenate([hi, mid, lo], axis=-1).astype(jnp.bfloat16)


def join3(value, count):
    parts = [value[..., k * count : (k + 1) * count].astype(jnp.float32) for k in range(3)]
    return (parts[0] + parts[1]) + parts[2]


def pack_weights(moments, pieces, width):
    lead = moments.shape[:-2]
    flat = moments.reshape(lead + (moments.shape[-2] * moments.shape[-1],))
    packed = jnp.concatenate([split3(flat), pieces.astype(jnp.bfloat16)], axis=-1)
    return jnp.pad(packed, [(0, 0)] * len(lead) + [(0, width - packed.shape[-1])])


def unpack_weights(packed, n_piece, n_moment):
    count = n_piece * n_moment
    lead = packed.shape[:-1]
    moments = join3(packed[..., : 3 * count], count).reshape(lead + (n_piece, n_moment))
    pieces = packed[..., 3 * count : 3 * count + n_piece].astype(jnp.int32)
    return moments, pieces


def face_weights(moments, pieces, tables):
    n_code = tables.shape[1]
    onehot = (pieces[..., None] == jnp.arange(n_code, dtype=jnp.int32)).astype(jnp.float32)
    spread = jnp.sum(onehot[..., :, None] * moments[..., None, :], axis=-3)
    lead = spread.shape[:-3]
    flat = spread.reshape(lead + (-1,))
    return jnp.dot(flat, tables.reshape(-1, tables.shape[-1]), precision=lax.Precision.HIGHEST)


def tap_sum(weights, padded, row0, col0, nrow, ncol, offsets, taps):
    total = None
    for tap in taps:
        dr, dc = offsets[tap]
        piece = lax.slice(
            padded, (3 + row0 + dr, 3 + col0 + dc, 0), (3 + row0 + dr + nrow, 3 + col0 + dc + ncol, padded.shape[2])
        )
        term = weights[:, :, tap][:, :, None] * piece.astype(jnp.float32)
        total = term if total is None else total + term
    return total


def face_weights_cells(moments, pieces, tables):
    n_row, n_col = moments.shape[:2]
    n_code = tables.shape[1]
    m_t = jnp.transpose(moments, (2, 3, 4, 0, 1)).reshape(moments.shape[2:] + (n_row * n_col,))
    p_t = jnp.transpose(pieces, (2, 3, 0, 1)).reshape(pieces.shape[2:] + (n_row * n_col,))
    onehot = (p_t[:, :, None, :] == jnp.arange(n_code, dtype=jnp.int32)[None, None, :, None]).astype(jnp.float32)
    spread = jnp.sum(onehot[:, :, :, None, :] * m_t[:, :, None, :, :], axis=1)
    flat = spread.reshape(-1, n_row * n_col).T
    scaled = jnp.round(tables * 24.0).reshape(-1, tables.shape[-1])
    weights = jnp.dot(flat, scaled, precision=lax.Precision.HIGH) / 24.0
    return weights.reshape(n_row, n_col, tables.shape[-1])


def tap_kernel(offsets, chunk, w_ref, p_ref, t_ref, o_ref, s_ref):
    s_ref[...] = p_ref[...].astype(jnp.float32)
    rows, cols, width = t_ref.shape

    def row(i, carry):
        for start in range(0, width, chunk):
            lanes = pl.ds(start, chunk)
            acc = t_ref[i, :, lanes].astype(jnp.float32)
            for tap, (dr, dc) in enumerate(offsets):
                w = w_ref[i, :, tap : tap + 1]
                acc = acc + w * s_ref[i + 3 + dr, pl.ds(3 + dc, cols), lanes]
            o_ref[i, :, lanes] = acc.astype(o_ref.dtype)
        return carry

    lax.fori_loop(0, rows, row, 0)


def apply_taps(weights, padded, tracer, offsets):
    return pl.pallas_call(
        functools.partial(tap_kernel, offsets, tracer.shape[2]),
        out_shape=jax.ShapeDtypeStruct(tracer.shape, jnp.bfloat16),
        scratch_shapes=[pltpu.VMEM(padded.shape, jnp.float32)],
        interpret=INTERPRET,
    )(weights, padded, tracer)


def local(tracer, moments, pieces, cell_area):
    rows = tracer.shape[0]
    cols = tracer.shape[1]
    width = tracer.shape[2]
    n_piece = moments.shape[3]
    n_moment = moments.shape[4]
    np_tables, offsets = face_tables()
    tables = jnp.asarray(np_tables, jnp.float32)
    west_taps = [t for t in range(len(offsets)) if np.abs(np_tables[0, ..., t]).sum() > 0]
    south_taps = [t for t in range(len(offsets)) if np.abs(np_tables[2, ..., t]).sum() > 0]

    west_pack = pack_weights(moments[0][:, cols - 1], pieces[0][:, cols - 1], width)[:, None]
    from_west = from_prev(jnp.concatenate([tracer[:, cols - 3 :], west_pack], axis=1), "tile", True)
    from_east = from_next(tracer[:, :3], "tile", True)
    wide = jnp.concatenate([from_west[:, :3], tracer, from_east], axis=1)
    south_pack = jnp.pad(
        pack_weights(moments[1][rows - 1], pieces[1][rows - 1], width), ((3, 3), (0, 0))
    )[None]
    from_south = from_prev(jnp.concatenate([wide[rows - 3 :], south_pack], axis=0), "panel", False)
    from_north = from_next(wide[:3], "panel", False)
    padded = jnp.concatenate([from_south[:3], wide, from_north], axis=0)

    is_top = lax.axis_index("panel") == lax.axis_size("panel") - 1
    last_row = jnp.arange(rows) == rows - 1
    row_mask = jnp.where(jnp.logical_and(last_row, is_top), 0.0, 1.0).astype(jnp.float32)
    north_m = moments[1] * row_mask[:, None, None, None]
    zero_col = jnp.zeros_like(moments[0][:, :1])
    zero_row = jnp.zeros_like(moments[1][:1])
    face_m = jnp.stack(
        [
            jnp.concatenate([zero_col, moments[0][:, : cols - 1]], axis=1),
            moments[0],
            jnp.concatenate([zero_row, north_m[: rows - 1]], axis=0),
            north_m,
        ],
        axis=2,
    )
    face_p = jnp.stack(
        [
            jnp.concatenate([pieces[0][:, :1], pieces[0][:, : cols - 1]], axis=1),
            pieces[0],
            jnp.concatenate([pieces[1][:1], pieces[1][: rows - 1]], axis=0),
            pieces[1],
        ],
        axis=2,
    )
    weights = face_weights_cells(face_m, face_p, tables)
    weights = lax.optimization_barrier(weights)

    west_m, west_p = unpack_weights(from_west[:, 3], n_piece, n_moment)
    south_m, south_p = unpack_weights(from_south[3, 3 : 3 + cols], n_piece, n_moment)
    west_fix = face_weights(west_m[:, None], west_p[:, None], tables[:1])
    south_fix = face_weights(south_m[:, None], south_p[:, None], tables[2:3])
    weights = weights + jnp.pad(west_fix[:, None], ((0, 0), (0, cols - 1), (0, 0)))
    weights = weights + jnp.pad(south_fix[None], ((0, rows - 1), (0, 0), (0, 0)))
    weights = weights / cell_area[:, :, None]
    return apply_taps(weights, padded, tracer, offsets)


def solution(mesh):
    in_specs = (
        P("panel", "tile", None),
        P(None, "panel", "tile", None, None),
        P(None, "panel", "tile", None),
        P("panel", "tile"),
    )
    out_specs = P("panel", "tile", None)
    return jax.shard_map(local, mesh=mesh, in_specs=in_specs, out_specs=out_specs, check_vma=False)
```

```python
import functools
import math

import jax
import jax.numpy as jnp
import numpy as np
from jax import lax
from jax.experimental import pallas as pl
from jax.experimental.pallas import tpu as pltpu
from jax.sharding import PartitionSpec as P


INTERPRET = False


def from_prev(value, axis, wrap):
    size = lax.axis_size(axis)
    pairs = [(i, (i + 1) % size) for i in range(size if wrap else size - 1)]
    return lax.ppermute(value, axis, pairs)


def from_next(value, axis, wrap):
    size = lax.axis_size(axis)
    pairs = [((i + 1) % size, i) for i in range(size if wrap else size - 1)]
    return lax.ppermute(value, axis, pairs)


def stencil_table():
    stencil = np.zeros((6, 3, 3))
    stencil[0, 1, 1] = 7.0 / 6.0
    stencil[0, 1, 0] = -1.0 / 24.0
    stencil[0, 1, 2] = -1.0 / 24.0
    stencil[0, 0, 1] = -1.0 / 24.0
    stencil[0, 2, 1] = -1.0 / 24.0
    stencil[1, 1, 2] = 0.5
    stencil[1, 1, 0] = -0.5
    stencil[2, 2, 1] = 0.5
    stencil[2, 0, 1] = -0.5
    stencil[3, 1, 2] = 0.5
    stencil[3, 1, 0] = 0.5
    stencil[3, 1, 1] = -1.0
    stencil[4, 2, 2] = 0.25
    stencil[4, 2, 0] = -0.25
    stencil[4, 0, 2] = -0.25
    stencil[4, 0, 0] = 0.25
    stencil[5, 2, 1] = 0.5
    stencil[5, 0, 1] = 0.5
    stencil[5, 1, 1] = -1.0
    return stencil


def face_tables():
    stencil = stencil_table()
    tables = np.zeros((4, 12, 6, 7, 7))
    for face, (direction, shift_row, shift_col, sign) in enumerate(
        ((0, 0, -1, 1.0), (0, 0, 0, -1.0), (1, -1, 0, 1.0), (1, 0, 0, -1.0))
    ):
        for code in range(12):
            if direction == 0:
                row_off, col_off = code // 4 - 1, code % 4 - 1
            else:
                row_off, col_off = code % 4 - 1, code // 4 - 1
            for inner_row in range(-1, 2):
                for inner_col in range(-1, 2):
                    r = row_off + inner_row + shift_row + 3
                    c = col_off + inner_col + shift_col + 3
                    tables[face, code, :, r, c] += sign * stencil[:, inner_row + 1, inner_col + 1]
    tables = tables.reshape(4, 12, 6, 49)
    used = np.nonzero(np.abs(tables).sum(axis=(0, 1, 2)) > 0)[0]
    return tables[..., used], [(int(t) // 7 - 3, int(t) % 7 - 3) for t in used]


def summed_moments(pieces, moments):
    codes = jnp.arange(12, dtype=jnp.int32)
    onehot = (pieces[..., None] == codes).astype(jnp.float32)
    return jnp.einsum("...ko,...km->...om", onehot, moments, precision=lax.Precision.HIGHEST)


def split3(value):
    hi = lax.reduce_precision(value, exponent_bits=8, mantissa_bits=7)
    rest = value - hi
    mid = lax.reduce_precision(rest, exponent_bits=8, mantissa_bits=7)
    lo = rest - mid
    return jnp.concatenate([hi, mid, lo], axis=-1).astype(jnp.bfloat16)


def join3(value, count):
    parts = [value[..., k * count : (k + 1) * count].astype(jnp.float32) for k in range(3)]
    return (parts[0] + parts[1]) + parts[2]


def pack_weights(moments, pieces, width):
    lead = moments.shape[:-2]
    flat = moments.reshape(lead + (moments.shape[-2] * moments.shape[-1],))
    packed = jnp.concatenate([split3(flat), pieces.astype(jnp.bfloat16)], axis=-1)
    return jnp.pad(packed, [(0, 0)] * len(lead) + [(0, width - packed.shape[-1])])


def unpack_weights(packed, n_piece, n_moment):
    count = n_piece * n_moment
    lead = packed.shape[:-1]
    moments = join3(packed[..., : 3 * count], count).reshape(lead + (n_piece, n_moment))
    pieces = packed[..., 3 * count : 3 * count + n_piece].astype(jnp.int32)
    return moments, pieces


def face_weights(moments, pieces, tables):
    n_code = tables.shape[1]
    onehot = (pieces[..., None] == jnp.arange(n_code, dtype=jnp.int32)).astype(jnp.float32)
    spread = jnp.sum(onehot[..., :, None] * moments[..., None, :], axis=-3)
    lead = spread.shape[:-3]
    flat = spread.reshape(lead + (-1,))
    return jnp.dot(flat, tables.reshape(-1, tables.shape[-1]), precision=lax.Precision.HIGHEST)


def tap_sum(weights, padded, row0, col0, nrow, ncol, offsets, taps):
    total = None
    for tap in taps:
        dr, dc = offsets[tap]
        piece = lax.slice(
            padded, (3 + row0 + dr, 3 + col0 + dc, 0), (3 + row0 + dr + nrow, 3 + col0 + dc + ncol, padded.shape[2])
        )
        term = weights[:, :, tap][:, :, None] * piece.astype(jnp.float32)
        total = term if total is None else total + term
    return total


def face_weights_cells(moments, pieces, tables):
    n_row, n_col = moments.shape[:2]
    n_code = tables.shape[1]
    m_t = jnp.transpose(moments, (2, 3, 4, 0, 1)).reshape(moments.shape[2:] + (n_row * n_col,))
    p_t = jnp.transpose(pieces, (2, 3, 0, 1)).reshape(pieces.shape[2:] + (n_row * n_col,))
    onehot = (p_t[:, :, None, :] == jnp.arange(n_code, dtype=jnp.int32)[None, None, :, None]).astype(jnp.float32)
    spread = jnp.sum(onehot[:, :, :, None, :] * m_t[:, :, None, :, :], axis=1)
    flat = spread.reshape(-1, n_row * n_col).T
    scaled = jnp.round(tables * 24.0).reshape(-1, tables.shape[-1])
    weights = jnp.dot(flat, scaled, precision=lax.Precision.HIGH) / 24.0
    return weights.reshape(n_row, n_col, tables.shape[-1])


def tap_kernel(offsets, base, w_ref, south_ref, t_ref, north_ref, west_ref, east_ref, o_ref, s_ref):
    rows, cols, width = t_ref.shape
    halo = north_ref.shape[0]
    f32 = jnp.float32
    s_ref[0:halo, base : base + cols] = south_ref[0:halo].astype(f32)
    s_ref[halo : halo + rows, base : base + cols] = t_ref[...].astype(f32)
    s_ref[halo + rows :, base : base + cols] = north_ref[...].astype(f32)
    s_ref[:, base - halo : base] = west_ref[:, 0:halo].astype(f32)
    s_ref[:, base + cols : base + cols + halo] = east_ref[...].astype(f32)

    def row(i, carry):
        acc = s_ref[i + halo, pl.ds(base, cols), :]
        for tap, (dr, dc) in enumerate(offsets):
            w = w_ref[i, :, tap : tap + 1]
            acc = acc + w * s_ref[i + halo + dr, pl.ds(base + dc, cols), :]
        o_ref[i] = acc.astype(o_ref.dtype)
        return carry

    lax.fori_loop(0, rows, row, 0)


def apply_taps(weights, from_south, tracer, from_north, from_west, from_east, offsets):
    rows, cols, width = tracer.shape
    halo = from_north.shape[0]
    base = 8
    return pl.pallas_call(
        functools.partial(tap_kernel, offsets, base),
        out_shape=jax.ShapeDtypeStruct(tracer.shape, jnp.bfloat16),
        scratch_shapes=[pltpu.VMEM((rows + 2 * halo, base + cols + 8, width), jnp.float32)],
        interpret=INTERPRET,
    )(weights, from_south, tracer, from_north, from_west, from_east)


def local(tracer, moments, pieces, cell_area):
    rows = tracer.shape[0]
    cols = tracer.shape[1]
    width = tracer.shape[2]
    n_piece = moments.shape[3]
    n_moment = moments.shape[4]
    np_tables, offsets = face_tables()
    tables = jnp.asarray(np_tables, jnp.float32)
    west_taps = [t for t in range(len(offsets)) if np.abs(np_tables[0, ..., t]).sum() > 0]
    south_taps = [t for t in range(len(offsets)) if np.abs(np_tables[2, ..., t]).sum() > 0]

    south_pack = pack_weights(moments[1][rows - 1], pieces[1][rows - 1], width)[None]
    from_south = from_prev(jnp.concatenate([tracer[rows - 3 :], south_pack], axis=0), "panel", False)
    from_north = from_next(tracer[:3], "panel", False)
    tall = jnp.concatenate([from_south[:3], tracer, from_north], axis=0)
    west_pack = jnp.pad(
        pack_weights(moments[0][:, cols - 1], pieces[0][:, cols - 1], width), ((3, 3), (0, 0))
    )[:, None]
    from_west = from_prev(jnp.concatenate([tall[:, cols - 3 :], west_pack], axis=1), "tile", True)
    from_east = from_next(tall[:, :3], "tile", True)

    is_top = lax.axis_index("panel") == lax.axis_size("panel") - 1
    last_row = jnp.arange(rows) == rows - 1
    row_mask = jnp.where(jnp.logical_and(last_row, is_top), 0.0, 1.0).astype(jnp.float32)
    north_m = moments[1] * row_mask[:, None, None, None]
    zero_col = jnp.zeros_like(moments[0][:, :1])
    zero_row = jnp.zeros_like(moments[1][:1])
    face_m = jnp.stack(
        [
            jnp.concatenate([zero_col, moments[0][:, : cols - 1]], axis=1),
            moments[0],
            jnp.concatenate([zero_row, north_m[: rows - 1]], axis=0),
            north_m,
        ],
        axis=2,
    )
    face_p = jnp.stack(
        [
            jnp.concatenate([pieces[0][:, :1], pieces[0][:, : cols - 1]], axis=1),
            pieces[0],
            jnp.concatenate([pieces[1][:1], pieces[1][: rows - 1]], axis=0),
            pieces[1],
        ],
        axis=2,
    )
    weights = face_weights_cells(face_m, face_p, tables)
    weights = lax.optimization_barrier(weights)

    west_m, west_p = unpack_weights(from_west[3 : 3 + rows, 3], n_piece, n_moment)
    south_m, south_p = unpack_weights(from_south[3], n_piece, n_moment)
    west_fix = face_weights(west_m[:, None], west_p[:, None], tables[:1])
    south_fix = face_weights(south_m[:, None], south_p[:, None], tables[2:3])
    weights = weights + jnp.pad(west_fix[:, None], ((0, 0), (0, cols - 1), (0, 0)))
    weights = weights + jnp.pad(south_fix[None], ((0, rows - 1), (0, 0), (0, 0)))
    weights = weights / cell_area[:, :, None]
    return apply_taps(weights, from_south, tracer, from_north, from_west, from_east, offsets)


def solution(mesh):
    in_specs = (
        P("panel", "tile", None),
        P(None, "panel", "tile", None, None),
        P(None, "panel", "tile", None),
        P("panel", "tile"),
    )
    out_specs = P("panel", "tile", None)
    return jax.shard_map(local, mesh=mesh, in_specs=in_specs, out_specs=out_specs, check_vma=False)
```

```python
import functools
import math

import jax
import jax.numpy as jnp
import numpy as np
from jax import lax
from jax.experimental import pallas as pl
from jax.experimental.pallas import tpu as pltpu
from jax.sharding import PartitionSpec as P


INTERPRET = False


def from_prev(value, axis, wrap):
    size = lax.axis_size(axis)
    pairs = [(i, (i + 1) % size) for i in range(size if wrap else size - 1)]
    return lax.ppermute(value, axis, pairs)


def from_next(value, axis, wrap):
    size = lax.axis_size(axis)
    pairs = [((i + 1) % size, i) for i in range(size if wrap else size - 1)]
    return lax.ppermute(value, axis, pairs)


def stencil_table():
    stencil = np.zeros((6, 3, 3))
    stencil[0, 1, 1] = 7.0 / 6.0
    stencil[0, 1, 0] = -1.0 / 24.0
    stencil[0, 1, 2] = -1.0 / 24.0
    stencil[0, 0, 1] = -1.0 / 24.0
    stencil[0, 2, 1] = -1.0 / 24.0
    stencil[1, 1, 2] = 0.5
    stencil[1, 1, 0] = -0.5
    stencil[2, 2, 1] = 0.5
    stencil[2, 0, 1] = -0.5
    stencil[3, 1, 2] = 0.5
    stencil[3, 1, 0] = 0.5
    stencil[3, 1, 1] = -1.0
    stencil[4, 2, 2] = 0.25
    stencil[4, 2, 0] = -0.25
    stencil[4, 0, 2] = -0.25
    stencil[4, 0, 0] = 0.25
    stencil[5, 2, 1] = 0.5
    stencil[5, 0, 1] = 0.5
    stencil[5, 1, 1] = -1.0
    return stencil


def face_tables():
    stencil = stencil_table()
    tables = np.zeros((4, 12, 6, 7, 7))
    for face, (direction, shift_row, shift_col, sign) in enumerate(
        ((0, 0, -1, 1.0), (0, 0, 0, -1.0), (1, -1, 0, 1.0), (1, 0, 0, -1.0))
    ):
        for code in range(12):
            if direction == 0:
                row_off, col_off = code // 4 - 1, code % 4 - 1
            else:
                row_off, col_off = code % 4 - 1, code // 4 - 1
            for inner_row in range(-1, 2):
                for inner_col in range(-1, 2):
                    r = row_off + inner_row + shift_row + 3
                    c = col_off + inner_col + shift_col + 3
                    tables[face, code, :, r, c] += sign * stencil[:, inner_row + 1, inner_col + 1]
    tables = tables.reshape(4, 12, 6, 49)
    used = np.nonzero(np.abs(tables).sum(axis=(0, 1, 2)) > 0)[0]
    return tables[..., used], [(int(t) // 7 - 3, int(t) % 7 - 3) for t in used]


def summed_moments(pieces, moments):
    codes = jnp.arange(12, dtype=jnp.int32)
    onehot = (pieces[..., None] == codes).astype(jnp.float32)
    return jnp.einsum("...ko,...km->...om", onehot, moments, precision=lax.Precision.HIGHEST)


def split3(value):
    hi = lax.reduce_precision(value, exponent_bits=8, mantissa_bits=7)
    rest = value - hi
    mid = lax.reduce_precision(rest, exponent_bits=8, mantissa_bits=7)
    lo = rest - mid
    return jnp.concatenate([hi, mid, lo], axis=-1).astype(jnp.bfloat16)


def join3(value, count):
    parts = [value[..., k * count : (k + 1) * count].astype(jnp.float32) for k in range(3)]
    return (parts[0] + parts[1]) + parts[2]


def pack_weights(moments, pieces, width):
    lead = moments.shape[:-2]
    flat = moments.reshape(lead + (moments.shape[-2] * moments.shape[-1],))
    packed = jnp.concatenate([split3(flat), pieces.astype(jnp.bfloat16)], axis=-1)
    return jnp.pad(packed, [(0, 0)] * len(lead) + [(0, width - packed.shape[-1])])


def unpack_weights(packed, n_piece, n_moment):
    count = n_piece * n_moment
    lead = packed.shape[:-1]
    moments = join3(packed[..., : 3 * count], count).reshape(lead + (n_piece, n_moment))
    pieces = packed[..., 3 * count : 3 * count + n_piece].astype(jnp.int32)
    return moments, pieces


def face_weights(moments, pieces, tables):
    n_code = tables.shape[1]
    onehot = (pieces[..., None] == jnp.arange(n_code, dtype=jnp.int32)).astype(jnp.float32)
    spread = jnp.sum(onehot[..., :, None] * moments[..., None, :], axis=-3)
    lead = spread.shape[:-3]
    flat = spread.reshape(lead + (-1,))
    return jnp.dot(flat, tables.reshape(-1, tables.shape[-1]), precision=lax.Precision.HIGHEST)


def tap_sum(weights, padded, row0, col0, nrow, ncol, offsets, taps):
    total = None
    for tap in taps:
        dr, dc = offsets[tap]
        piece = lax.slice(
            padded, (3 + row0 + dr, 3 + col0 + dc, 0), (3 + row0 + dr + nrow, 3 + col0 + dc + ncol, padded.shape[2])
        )
        term = weights[:, :, tap][:, :, None] * piece.astype(jnp.float32)
        total = term if total is None else total + term
    return total


def face_weights_cells(moments, pieces, tables):
    n_row, n_col = moments.shape[:2]
    n_code = tables.shape[1]
    m_t = jnp.transpose(moments, (2, 3, 4, 0, 1)).reshape(moments.shape[2:] + (n_row * n_col,))
    p_t = jnp.transpose(pieces, (2, 3, 0, 1)).reshape(pieces.shape[2:] + (n_row * n_col,))
    onehot = (p_t[:, :, None, :] == jnp.arange(n_code, dtype=jnp.int32)[None, None, :, None]).astype(jnp.float32)
    spread = jnp.sum(onehot[:, :, :, None, :] * m_t[:, :, None, :, :], axis=1)
    flat = spread.reshape(-1, n_row * n_col).T
    scaled = jnp.round(tables * 24.0).reshape(-1, tables.shape[-1])
    weights = jnp.dot(flat, scaled, precision=lax.Precision.HIGH) / 24.0
    return weights.reshape(n_row, n_col, tables.shape[-1])


def tap_kernel(offsets, base, w_ref, south_ref, t_ref, north_ref, west_ref, east_ref, o_ref, s_ref):
    rows, cols, width = t_ref.shape
    halo = north_ref.shape[0]
    f32 = jnp.float32
    s_ref[0:halo, base : base + cols] = south_ref[0:halo].astype(f32)
    s_ref[halo : halo + rows, base : base + cols] = t_ref[...].astype(f32)
    s_ref[halo + rows :, base : base + cols] = north_ref[...].astype(f32)
    s_ref[:, base - halo : base] = west_ref[:, 0:halo].astype(f32)
    s_ref[:, base + cols : base + cols + halo] = east_ref[...].astype(f32)

    def row(i, carry):
        acc = s_ref[i + halo, pl.ds(base, cols), :]
        for tap, (dr, dc) in enumerate(offsets):
            w = w_ref[i, :, tap : tap + 1]
            acc = acc + w * s_ref[i + halo + dr, pl.ds(base + dc, cols), :]
        o_ref[i] = acc.astype(o_ref.dtype)
        return carry

    lax.fori_loop(0, rows, row, 0)


def edge_kernel(offsets, base, w_ref, south_ref, t_ref, north_ref, west_ref, east_ref, left_ref, right_ref, s_ref):
    rows, cols, width = t_ref.shape
    halo = north_ref.shape[0]
    f32 = jnp.float32
    s_ref[0:halo, base : base + cols] = south_ref[0:halo].astype(f32)
    s_ref[halo : halo + rows, base : base + cols] = t_ref[...].astype(f32)
    s_ref[halo + rows :, base : base + cols] = north_ref[...].astype(f32)
    s_ref[:, base - halo : base] = west_ref[:, 0:halo].astype(f32)
    s_ref[:, base + cols : base + cols + halo] = east_ref[...].astype(f32)

    def row(i, carry):
        for first, out_ref in ((0, left_ref), (cols - halo, right_ref)):
            acc = s_ref[i + halo, pl.ds(base + first, halo), :]
            for tap, (dr, dc) in enumerate(offsets):
                w = w_ref[i, first : first + halo, tap : tap + 1]
                acc = acc + w * s_ref[i + halo + dr, pl.ds(base + first + dc, halo), :]
            out_ref[i] = acc.astype(out_ref.dtype)
        return carry

    lax.fori_loop(0, rows, row, 0)


def edge_taps(weights, from_south, tracer, from_north, from_west, from_east, offsets):
    rows, cols, width = tracer.shape
    halo = from_north.shape[0]
    base = 8
    side = jax.ShapeDtypeStruct((rows, halo, width), jnp.bfloat16)
    return pl.pallas_call(
        functools.partial(edge_kernel, offsets, base),
        out_shape=(side, side),
        scratch_shapes=[pltpu.VMEM((rows + 2 * halo, base + cols + 8, width), jnp.float32)],
        interpret=INTERPRET,
    )(weights, from_south, tracer, from_north, from_west, from_east)


def apply_taps(weights, from_south, tracer, from_north, from_west, from_east, offsets):
    rows, cols, width = tracer.shape
    halo = from_north.shape[0]
    base = 8
    return pl.pallas_call(
        functools.partial(tap_kernel, offsets, base),
        out_shape=jax.ShapeDtypeStruct(tracer.shape, jnp.bfloat16),
        scratch_shapes=[pltpu.VMEM((rows + 2 * halo, base + cols + 8, width), jnp.float32)],
        interpret=INTERPRET,
    )(weights, from_south, tracer, from_north, from_west, from_east)


def local(tracer, moments, pieces, cell_area):
    rows = tracer.shape[0]
    cols = tracer.shape[1]
    width = tracer.shape[2]
    n_piece = moments.shape[3]
    n_moment = moments.shape[4]
    np_tables, offsets = face_tables()
    tables = jnp.asarray(np_tables, jnp.float32)
    west_taps = [t for t in range(len(offsets)) if np.abs(np_tables[0, ..., t]).sum() > 0]
    south_taps = [t for t in range(len(offsets)) if np.abs(np_tables[2, ..., t]).sum() > 0]

    south_pack = pack_weights(moments[1][rows - 1], pieces[1][rows - 1], width)[None]
    from_south = from_prev(jnp.concatenate([tracer[rows - 3 :], south_pack], axis=0), "panel", False)
    from_north = from_next(tracer[:3], "panel", False)
    tall = jnp.concatenate([from_south[:3], tracer, from_north], axis=0)
    west_pack = jnp.pad(
        pack_weights(moments[0][:, cols - 1], pieces[0][:, cols - 1], width), ((3, 3), (0, 0))
    )[:, None]
    from_west = from_prev(jnp.concatenate([tall[:, cols - 3 :], west_pack], axis=1), "tile", True)
    from_east = from_next(tall[:, :3], "tile", True)

    is_top = lax.axis_index("panel") == lax.axis_size("panel") - 1
    last_row = jnp.arange(rows) == rows - 1
    row_mask = jnp.where(jnp.logical_and(last_row, is_top), 0.0, 1.0).astype(jnp.float32)
    north_m = moments[1] * row_mask[:, None, None, None]
    zero_col = jnp.zeros_like(moments[0][:, :1])
    zero_row = jnp.zeros_like(moments[1][:1])
    face_m = jnp.stack(
        [
            jnp.concatenate([zero_col, moments[0][:, : cols - 1]], axis=1),
            moments[0],
            jnp.concatenate([zero_row, north_m[: rows - 1]], axis=0),
            north_m,
        ],
        axis=2,
    )
    face_p = jnp.stack(
        [
            jnp.concatenate([pieces[0][:, :1], pieces[0][:, : cols - 1]], axis=1),
            pieces[0],
            jnp.concatenate([pieces[1][:1], pieces[1][: rows - 1]], axis=0),
            pieces[1],
        ],
        axis=2,
    )
    weights = face_weights_cells(face_m, face_p, tables)
    weights = lax.optimization_barrier(weights)

    west_m, west_p = unpack_weights(from_west[3 : 3 + rows, 3], n_piece, n_moment)
    south_m, south_p = unpack_weights(from_south[3], n_piece, n_moment)
    west_fix = face_weights(west_m[:, None], west_p[:, None], tables[:1])
    south_fix = face_weights(south_m[:, None], south_p[:, None], tables[2:3])
    weights = weights + jnp.pad(south_fix[None], ((0, rows - 1), (0, 0), (0, 0)))
    inner_weights = weights / cell_area[:, :, None]
    weights = weights + jnp.pad(west_fix[:, None], ((0, 0), (0, cols - 1), (0, 0)))
    weights = weights / cell_area[:, :, None]
    no_west = jnp.zeros_like(from_west)
    no_east = jnp.zeros_like(from_east)
    inner = apply_taps(inner_weights, from_south, tracer, from_north, no_west, no_east, offsets)
    left, right = edge_taps(weights, from_south, tracer, from_north, from_west, from_east, offsets)
    return jnp.concatenate([left, inner[:, 3 : cols - 3], right], axis=1)


def solution(mesh):
    in_specs = (
        P("panel", "tile", None),
        P(None, "panel", "tile", None, None),
        P(None, "panel", "tile", None),
        P("panel", "tile"),
    )
    out_specs = P("panel", "tile", None)
    return jax.shard_map(local, mesh=mesh, in_specs=in_specs, out_specs=out_specs, check_vma=False)
```

```python
import functools
import math

import jax
import jax.numpy as jnp
import numpy as np
from jax import lax
from jax.experimental import pallas as pl
from jax.experimental.pallas import tpu as pltpu
from jax.sharding import PartitionSpec as P


INTERPRET = False


def from_prev(value, axis, wrap):
    size = lax.axis_size(axis)
    pairs = [(i, (i + 1) % size) for i in range(size if wrap else size - 1)]
    return lax.ppermute(value, axis, pairs)


def from_next(value, axis, wrap):
    size = lax.axis_size(axis)
    pairs = [((i + 1) % size, i) for i in range(size if wrap else size - 1)]
    return lax.ppermute(value, axis, pairs)


def stencil_table():
    stencil = np.zeros((6, 3, 3))
    stencil[0, 1, 1] = 7.0 / 6.0
    stencil[0, 1, 0] = -1.0 / 24.0
    stencil[0, 1, 2] = -1.0 / 24.0
    stencil[0, 0, 1] = -1.0 / 24.0
    stencil[0, 2, 1] = -1.0 / 24.0
    stencil[1, 1, 2] = 0.5
    stencil[1, 1, 0] = -0.5
    stencil[2, 2, 1] = 0.5
    stencil[2, 0, 1] = -0.5
    stencil[3, 1, 2] = 0.5
    stencil[3, 1, 0] = 0.5
    stencil[3, 1, 1] = -1.0
    stencil[4, 2, 2] = 0.25
    stencil[4, 2, 0] = -0.25
    stencil[4, 0, 2] = -0.25
    stencil[4, 0, 0] = 0.25
    stencil[5, 2, 1] = 0.5
    stencil[5, 0, 1] = 0.5
    stencil[5, 1, 1] = -1.0
    return stencil


def face_tables():
    stencil = stencil_table()
    tables = np.zeros((4, 12, 6, 7, 7))
    for face, (direction, shift_row, shift_col, sign) in enumerate(
        ((0, 0, -1, 1.0), (0, 0, 0, -1.0), (1, -1, 0, 1.0), (1, 0, 0, -1.0))
    ):
        for code in range(12):
            if direction == 0:
                row_off, col_off = code // 4 - 1, code % 4 - 1
            else:
                row_off, col_off = code % 4 - 1, code // 4 - 1
            for inner_row in range(-1, 2):
                for inner_col in range(-1, 2):
                    r = row_off + inner_row + shift_row + 3
                    c = col_off + inner_col + shift_col + 3
                    tables[face, code, :, r, c] += sign * stencil[:, inner_row + 1, inner_col + 1]
    tables = tables.reshape(4, 12, 6, 49)
    used = np.nonzero(np.abs(tables).sum(axis=(0, 1, 2)) > 0)[0]
    return tables[..., used], [(int(t) // 7 - 3, int(t) % 7 - 3) for t in used]


def summed_moments(pieces, moments):
    codes = jnp.arange(12, dtype=jnp.int32)
    onehot = (pieces[..., None] == codes).astype(jnp.float32)
    return jnp.einsum("...ko,...km->...om", onehot, moments, precision=lax.Precision.HIGHEST)


def split3(value):
    hi = lax.reduce_precision(value, exponent_bits=8, mantissa_bits=7)
    rest = value - hi
    mid = lax.reduce_precision(rest, exponent_bits=8, mantissa_bits=7)
    lo = rest - mid
    return jnp.concatenate([hi, mid, lo], axis=-1).astype(jnp.bfloat16)


def join3(value, count):
    parts = [value[..., k * count : (k + 1) * count].astype(jnp.float32) for k in range(3)]
    return (parts[0] + parts[1]) + parts[2]


def pack_weights(moments, pieces, width):
    lead = moments.shape[:-2]
    flat = moments.reshape(lead + (moments.shape[-2] * moments.shape[-1],))
    packed = jnp.concatenate([split3(flat), pieces.astype(jnp.bfloat16)], axis=-1)
    return jnp.pad(packed, [(0, 0)] * len(lead) + [(0, width - packed.shape[-1])])


def unpack_weights(packed, n_piece, n_moment):
    count = n_piece * n_moment
    lead = packed.shape[:-1]
    moments = join3(packed[..., : 3 * count], count).reshape(lead + (n_piece, n_moment))
    pieces = packed[..., 3 * count : 3 * count + n_piece].astype(jnp.int32)
    return moments, pieces


def face_weights(moments, pieces, tables):
    n_code = tables.shape[1]
    onehot = (pieces[..., None] == jnp.arange(n_code, dtype=jnp.int32)).astype(jnp.float32)
    spread = jnp.sum(onehot[..., :, None] * moments[..., None, :], axis=-3)
    lead = spread.shape[:-3]
    flat = spread.reshape(lead + (-1,))
    return jnp.dot(flat, tables.reshape(-1, tables.shape[-1]), precision=lax.Precision.HIGHEST)


def tap_sum(weights, padded, row0, col0, nrow, ncol, offsets, taps):
    total = None
    for tap in taps:
        dr, dc = offsets[tap]
        piece = lax.slice(
            padded, (3 + row0 + dr, 3 + col0 + dc, 0), (3 + row0 + dr + nrow, 3 + col0 + dc + ncol, padded.shape[2])
        )
        term = weights[:, :, tap][:, :, None] * piece.astype(jnp.float32)
        total = term if total is None else total + term
    return total


def face_weights_cells(moments, pieces, tables):
    n_row, n_col = moments.shape[:2]
    n_code = tables.shape[1]
    m_t = jnp.transpose(moments, (2, 3, 4, 0, 1)).reshape(moments.shape[2:] + (n_row * n_col,))
    p_t = jnp.transpose(pieces, (2, 3, 0, 1)).reshape(pieces.shape[2:] + (n_row * n_col,))
    onehot = (p_t[:, :, None, :] == jnp.arange(n_code, dtype=jnp.int32)[None, None, :, None]).astype(jnp.float32)
    spread = jnp.sum(onehot[:, :, :, None, :] * m_t[:, :, None, :, :], axis=1)
    flat = spread.reshape(-1, n_row * n_col).T
    scaled = jnp.round(tables * 24.0).reshape(-1, tables.shape[-1])
    weights = jnp.dot(flat, scaled, precision=lax.Precision.HIGH) / 24.0
    return weights.reshape(n_row, n_col, tables.shape[-1])


def tap_kernel(offsets, base, w_ref, south_ref, t_ref, north_ref, west_ref, east_ref, o_ref, s_ref):
    rows, cols, width = t_ref.shape
    halo = north_ref.shape[0]
    f32 = jnp.float32
    s_ref[0:halo, base : base + cols] = south_ref[0:halo].astype(f32)
    s_ref[halo : halo + rows, base : base + cols] = t_ref[...].astype(f32)
    s_ref[halo + rows :, base : base + cols] = north_ref[...].astype(f32)
    s_ref[:, base - halo : base] = west_ref[:, 0:halo].astype(f32)
    s_ref[:, base + cols : base + cols + halo] = east_ref[...].astype(f32)

    for i in range(rows):
        acc = s_ref[i + halo, pl.ds(base, cols), :]
        for tap, (dr, dc) in enumerate(offsets):
            w = w_ref[i, :, tap : tap + 1]
            acc = acc + w * s_ref[i + halo + dr, pl.ds(base + dc, cols), :]
        o_ref[i] = acc.astype(o_ref.dtype)


def apply_taps(weights, from_south, tracer, from_north, from_west, from_east, offsets):
    rows, cols, width = tracer.shape
    halo = from_north.shape[0]
    base = 8
    return pl.pallas_call(
        functools.partial(tap_kernel, offsets, base),
        out_shape=jax.ShapeDtypeStruct(tracer.shape, jnp.bfloat16),
        scratch_shapes=[pltpu.VMEM((rows + 2 * halo, base + cols + 8, width), jnp.float32)],
        interpret=INTERPRET,
    )(weights, from_south, tracer, from_north, from_west, from_east)


def local(tracer, moments, pieces, cell_area):
    rows = tracer.shape[0]
    cols = tracer.shape[1]
    width = tracer.shape[2]
    n_piece = moments.shape[3]
    n_moment = moments.shape[4]
    np_tables, offsets = face_tables()
    tables = jnp.asarray(np_tables, jnp.float32)
    west_taps = [t for t in range(len(offsets)) if np.abs(np_tables[0, ..., t]).sum() > 0]
    south_taps = [t for t in range(len(offsets)) if np.abs(np_tables[2, ..., t]).sum() > 0]

    south_pack = pack_weights(moments[1][rows - 1], pieces[1][rows - 1], width)[None]
    from_south = from_prev(jnp.concatenate([tracer[rows - 3 :], south_pack], axis=0), "panel", False)
    from_north = from_next(tracer[:3], "panel", False)
    tall = jnp.concatenate([from_south[:3], tracer, from_north], axis=0)
    west_pack = jnp.pad(
        pack_weights(moments[0][:, cols - 1], pieces[0][:, cols - 1], width), ((3, 3), (0, 0))
    )[:, None]
    from_west = from_prev(jnp.concatenate([tall[:, cols - 3 :], west_pack], axis=1), "tile", True)
    from_east = from_next(tall[:, :3], "tile", True)

    is_top = lax.axis_index("panel") == lax.axis_size("panel") - 1
    last_row = jnp.arange(rows) == rows - 1
    row_mask = jnp.where(jnp.logical_and(last_row, is_top), 0.0, 1.0).astype(jnp.float32)
    north_m = moments[1] * row_mask[:, None, None, None]
    zero_col = jnp.zeros_like(moments[0][:, :1])
    zero_row = jnp.zeros_like(moments[1][:1])
    face_m = jnp.stack(
        [
            jnp.concatenate([zero_col, moments[0][:, : cols - 1]], axis=1),
            moments[0],
            jnp.concatenate([zero_row, north_m[: rows - 1]], axis=0),
            north_m,
        ],
        axis=2,
    )
    face_p = jnp.stack(
        [
            jnp.concatenate([pieces[0][:, :1], pieces[0][:, : cols - 1]], axis=1),
            pieces[0],
            jnp.concatenate([pieces[1][:1], pieces[1][: rows - 1]], axis=0),
            pieces[1],
        ],
        axis=2,
    )
    weights = face_weights_cells(face_m, face_p, tables)
    weights = lax.optimization_barrier(weights)

    west_m, west_p = unpack_weights(from_west[3 : 3 + rows, 3], n_piece, n_moment)
    south_m, south_p = unpack_weights(from_south[3], n_piece, n_moment)
    west_fix = face_weights(west_m[:, None], west_p[:, None], tables[:1])
    south_fix = face_weights(south_m[:, None], south_p[:, None], tables[2:3])
    weights = weights + jnp.pad(west_fix[:, None], ((0, 0), (0, cols - 1), (0, 0)))
    weights = weights + jnp.pad(south_fix[None], ((0, rows - 1), (0, 0), (0, 0)))
    weights = weights / cell_area[:, :, None]
    return apply_taps(weights, from_south, tracer, from_north, from_west, from_east, offsets)


def solution(mesh):
    in_specs = (
        P("panel", "tile", None),
        P(None, "panel", "tile", None, None),
        P(None, "panel", "tile", None),
        P("panel", "tile"),
    )
    out_specs = P("panel", "tile", None)
    return jax.shard_map(local, mesh=mesh, in_specs=in_specs, out_specs=out_specs, check_vma=False)
```
